256 devices in a mesh: role: 2 (over core), dp: 16 (over x, y), tensor: 8 (over z).
Axes of the slice: x: 4, y: 4, z: 8, core: 2. Of those that a mesh axis runs over, the one named last changes fastest.
Arguments:
- queries: bfloat16 [1024, 128, 576], P(('dp', 'tensor'), 'role'), may hold values from -13 to 13
- latent_cache: bfloat16 [512, 1024, 576], P(('dp', 'tensor')), may hold values from -4 to 4
- new_latent: bfloat16 [1024, 576], P(('dp', 'tensor')), may hold values from -9 to 9
- cache_lengths: int32 [512], P(('dp', 'tensor')), may hold values from 2 to 1024
- value_proj: bfloat16 [128, 512, 128], P(('role', 'tensor')), may hold values from -1 to 1
- out_proj: bfloat16 [16384, 7168], P(('role', 'tensor'), 'dp'), may hold values from -0.046875 to 0.046875
- residual: bfloat16 [1024, 7168], P(('role', 'tensor'), 'dp'), may hold values from -68 to 68
- norm_gain: bfloat16 [7168], replicated, may hold values from 0.5 to 1.5
- routes: int32 [1024, 8], P(('role', 'tensor')), may hold values from 0 to 15, all different within a row; in each aligned block of 64 rows (0 to 63, 64 to 127, ...) at most 40 rows name the same one
- gate_values: float32 [1024, 8], P(('role', 'tensor')), may hold values from 0.2 to 0.8
- tenant_ids: int32 [1024], P(('role', 'tensor')), may hold values from 0 to 2
- expert_gate_weight: bfloat16 [16, 7168, 2048], P('dp', None, ('role', 'tensor')), may hold values from -0.0625 to 0.0625
- expert_up_weight: bfloat16 [16, 7168, 2048], P('dp', None, ('role', 'tensor')), may hold values from -0.0625 to 0.0625
- expert_down_weight: bfloat16 [16, 2048, 7168], P('dp', ('role', 'tensor')), may hold values from -0.125 to 0.125
- left_delta_factor: bfloat16 [3, 16, 2048, 64], P(None, 'dp', ('role', 'tensor')), may hold values from -0.125 to 0.125
- factor_right: bfloat16 [3, 16, 64, 7168], P(None, 'dp'), may hold values from -0.75 to 0.75
Outputs:
- mixed: bfloat16 [1024, 7168], P(('role', 'tensor'), 'dp')
The draws below stay inside these ranges and needn't reach their ends.
Inputs may be any that keep to these rules, and one draw needn't show every extreme that they name: `routes`: in each aligned block of 64 tokens no expert is named by more than 40 of them.
All inputs are finite; a program needn't handle non-finite values.
Results may differ from the reference program's by a relative error of at most 0.008.
Values may be sent and summed in bfloat16 or wider, within the bound.
No kernel may reach another device: no remote copies, remote signals or barrier semaphores. Data moves between devices by JAX's collectives and lax.ppermute only.
A program may use at most 128 MiB of HBM per device.

```python
import math
import jax
import jax.numpy as jnp
import numpy as np
from jax import lax

D = 7168
H = 128
LAT = 512
ROPE = 64
VH = 128
FF = 2048
TOP = 8
EXPERTS = 16
RANK = 64
TEN = 3
CTX = 1024
SEQS = 512
TOKENS = 1024
TOK_GRP = 64
CAP = 40


def draw_latent_cache(key, part):
    width = LAT + ROPE
    values = jnp.clip(jax.random.normal(jax.random.fold_in(key, 1), (SEQS, CTX, width), jnp.float32), -4.0, 4.0)
    return values.astype(jnp.bfloat16)


def draw_queries(key, part):
    width = LAT + ROPE
    values = jnp.clip(jax.random.normal(jax.random.fold_in(key, 2), (TOKENS, H, width), jnp.float32), -4.0, 4.0)
    return values.astype(jnp.bfloat16)


def draw_residual(key, part):
    noise = jnp.clip(jax.random.normal(jax.random.fold_in(key, 3), (TOKENS, D), jnp.float32), -4.0, 4.0)
    column = jnp.arange(D, dtype=jnp.float32) / D
    row_scale = jnp.exp(jax.random.uniform(jax.random.fold_in(key, 4), (TOKENS, 1), jnp.float32, math.log(0.3), math.log(3.0)))
    col_scale = 0.3 * jnp.exp(column * math.log(10.0))
    values = noise * row_scale * col_scale[None, :]
    return values.astype(jnp.bfloat16)


def draw_cache_lengths(key, part):
    drawn = jax.random.randint(jax.random.fold_in(key, 5), (SEQS,), 2, CTX + 1, dtype=jnp.int32)
    offset = jax.random.randint(jax.random.fold_in(key, 6), (), 0, 4, dtype=jnp.int32)
    full = jnp.arange(SEQS, dtype=jnp.int32) % 4 == offset
    return jnp.where(full, CTX, drawn).astype(jnp.int32)


def plant(entries, own_key, low, high):
    spot = [jax.random.randint(jax.random.fold_in(own_key, axis), (), 0, length) for axis, length in enumerate(entries.shape)]
    longest = entries.shape.index(max(entries.shape))
    beside = spot[:longest] + [(spot[longest] + 1) % entries.shape[longest]] + spot[longest + 1:]
    return entries.at[tuple(spot)].set(low).at[tuple(beside)].set(high)


def levels(key, dims, pieces, smallest, largest):
    gain = 1.0
    for axis_at, parts in pieces:
        draws = jax.random.uniform(jax.random.fold_in(jax.random.fold_in(key, 6), axis_at), (parts,), jnp.float32, smallest / len(pieces), largest / len(pieces))
        gain = gain * jnp.repeat(jnp.exp(draws), dims[axis_at] // parts).reshape((-1,) + (1,) * (len(dims) - 1 - axis_at))
    return gain


def assign_block(key, own, number, rows, count, top, bound, slope):
    ranking = jax.random.permutation(key, count)
    crowded, usual = shares(count, rows * top, bound, slope, True), shares(count, rows * top, bound, slope, False)
    places = jnp.arange(count)

    def named(sizes, offset_by):
        used = int((sizes > 0).sum())
        fixed = max(1, used // 4)
        shifted = fixed + (places - fixed + offset_by * (used - fixed)) % max(1, count - fixed)
        return jnp.zeros((count,), jnp.int32).at[ranking[jnp.where(places < fixed, places, shifted)]].set(jnp.asarray(sizes, jnp.int32))

    sizes = jnp.where(number % 4 == 0, named(crowded, number // 4), named(usual, number - number // 4 - 1))
    mixed = jax.random.permutation(jax.random.fold_in(own, 3), count)
    source_of, sink = mixed[0:count // 2 * 2:2], mixed[1:count // 2 * 2:2]
    slack = jnp.minimum(sizes[source_of] - 1, bound - sizes[sink]) // 2
    slack = jnp.where((source_of == ranking[0]) | (sink == ranking[0]) | (sizes[sink] == 0), 0, jnp.maximum(slack, 0))
    shifted = jax.random.randint(jax.random.fold_in(own, 4), (count // 2,), 0, 1 << 20) % (slack + 1)
    sizes = sizes.at[source_of].add(-shifted).at[sink].add(shifted)
    members = jnp.searchsorted(jnp.cumsum(sizes), jnp.arange(rows * top), side="right").astype(jnp.int32)
    table = members.reshape(top, rows).T
    table = table[jax.random.permutation(jax.random.fold_in(own, 1), rows)]
    offset_by = jax.random.randint(jax.random.fold_in(own, 2), (rows, 1), 0, top)
    return jnp.take_along_axis(table, (jnp.arange(top)[None, :] + offset_by) % top, axis=1)


def shares(number_of, total, most, lean, full):
    weights = [(1 << 20) // math.isqrt(standing ** lean) + 1 for standing in range(1, number_of + 1)]
    largest = most if full else min(most, max(-(-total // number_of), total * weights[0] // sum(weights)))
    least = 1 if total - largest >= number_of - 1 else 0
    given, spare = [largest] + [least] * (number_of - 1), total - largest - least * (number_of - 1)
    while spare > 0:
        candidates = [i for i in range(1, number_of) if given[i] < largest] or [i for i in range(1, number_of) if given[i] < most]
        pool, left = sum([weights[i] for i in candidates]), spare
        for i in candidates:
            addition = min(most - given[i], max(1, left * weights[i] // pool), spare)
            given[i] = given[i] + addition
            spare = spare - addition
    return np.array(given)


def bell_draw(stream_key, extent, deviation, most, shards=(), kind=jnp.bfloat16):
    values = jax.random.normal(stream_key, extent, jnp.float32) * deviation
    if len(shards) > 0:
        values = levels(stream_key, extent, shards, -0.22, 0.18) * values
    return jnp.clip(values, min=-most, max=most).astype(kind)


def setup_inputs(seed: int = 0) -> dict:
    arg_keys = jax.random.split(jax.random.key(seed), 17)
    queries = draw_queries(jax.random.fold_in(arg_keys[16], 71), 0)
    latent_cache = draw_latent_cache(jax.random.fold_in(arg_keys[16], 71), 0)
    new_latent = bell_draw(arg_keys[2], (TOKENS, LAT + ROPE), 2.2, 9.0, ((0, 128),))
    cache_lengths = draw_cache_lengths(jax.random.fold_in(arg_keys[16], 71), 0)
    value_proj = bell_draw(arg_keys[4], (H, LAT, VH), (max(LAT // 16, 1)) ** -0.5, 1.0, ((0, 16),))
    out_proj = bell_draw(arg_keys[5], (H * VH, D), (H * VH) ** -0.5, 0.046875, ((0, 16), (1, 16)))
    residual = draw_residual(jax.random.fold_in(arg_keys[16], 71), 0)
    norm_gain = jnp.clip(1.0 + 0.1 * jax.random.normal(arg_keys[7], (D,), jnp.float32), 0.5, 1.5).astype(jnp.bfloat16)
    routes_keys = jax.random.split(jax.random.fold_in(arg_keys[8], 1), TOKENS // TOK_GRP)
    routes_turns = jax.random.permutation(jax.random.fold_in(arg_keys[8], 3), TOKENS // TOK_GRP)
    routes = jax.vmap(lambda own, number: assign_block(jax.random.fold_in(arg_keys[8], 2), own, number, TOK_GRP, EXPERTS, TOP, CAP, 2))(routes_keys, routes_turns).reshape((TOKENS, TOP))
    gate_values = jnp.clip(0.2 + 0.6 * jax.random.uniform(arg_keys[9], (TOKENS, TOP), jnp.float32) ** levels(arg_keys[9], (TOKENS, TOP), ((0, 16),), -0.2, 0.2), 0.2, 0.8)
    tenant_ids = plant(jax.random.randint(arg_keys[10], (TOKENS,), 0, TEN), jax.random.fold_in(arg_keys[10], 1), 0, TEN - 1).astype(jnp.int32)
    expert_gate_weight = bell_draw(arg_keys[11], (EXPERTS, D, FF), D ** -0.5, 0.0625, ((0, 16), (2, 16)))
    expert_up_weight = bell_draw(arg_keys[12], (EXPERTS, D, FF), D ** -0.5, 0.0625, ((0, 16), (2, 16)))
    expert_down_weight = bell_draw(arg_keys[13], (EXPERTS, FF, D), FF ** -0.5, 0.125, ((0, 16), (1, 16)))
    left_delta_factor = bell_draw(arg_keys[14], (TEN, EXPERTS, FF, RANK), FF ** -0.5, 0.125, ((1, 16), (2, 16)))
    factor_right = bell_draw(arg_keys[15], (TEN, EXPERTS, RANK, D), RANK ** -0.5, 0.75, ((1, 16),))
    return dict(queries=queries, latent_cache=latent_cache, new_latent=new_latent, cache_lengths=cache_lengths, value_proj=value_proj, out_proj=out_proj, residual=residual, norm_gain=norm_gain, routes=routes, gate_values=gate_values, tenant_ids=tenant_ids, expert_gate_weight=expert_gate_weight, expert_up_weight=expert_up_weight, expert_down_weight=expert_down_weight, left_delta_factor=left_delta_factor, factor_right=factor_right)


SCORE_SCALE = 0.07216878364870323
NORM_EPS = 1e-06

def attend_sequence(inputs):
    query_pair, cache_rows, fresh_rows, length = inputs
    keys = jnp.concatenate([cache_rows, fresh_rows], axis=0).astype(jnp.float32)
    scores = jnp.einsum('qhd,pd->qhp', query_pair.astype(jnp.float32), keys, precision=lax.Precision.HIGHEST) * SCORE_SCALE
    cached = jnp.arange(CTX, dtype=jnp.int32) < length
    cached = jnp.broadcast_to(cached[None, :], (2, CTX))
    causal = jnp.arange(2, dtype=jnp.int32)[:, None] >= jnp.arange(2, dtype=jnp.int32)[None, :]
    valid = jnp.concatenate([cached, causal], axis=1)
    scores = jnp.where(valid[:, None, :], scores, -jnp.inf)
    top = lax.optimization_barrier(jnp.max(scores, axis=2, keepdims=True))
    weights = jnp.exp(scores - top)
    total = lax.optimization_barrier(jnp.sum(weights, axis=2))
    rounded = lax.optimization_barrier(weights.astype(jnp.bfloat16)).astype(jnp.float32)
    summed = jnp.einsum('qhp,pd->qhd', rounded, keys[:, :LAT], precision=lax.Precision.HIGHEST)
    return (summed / total[..., None]).astype(jnp.bfloat16)

def reference(queries, latent_cache, new_latent, cache_lengths, value_proj, out_proj, residual, norm_gain, routes, gate_values, tenant_ids, expert_gate_weight, expert_up_weight, expert_down_weight, left_delta_factor, factor_right):
    width = LAT + ROPE
    attended = lax.map(attend_sequence, (queries.reshape(SEQS, 2, H, width), latent_cache, new_latent.reshape(SEQS, 2, width), cache_lengths))
    attended = attended.reshape(TOKENS, H, LAT)
    head_values = jnp.einsum('thl,hlv->thv', attended.astype(jnp.float32), value_proj.astype(jnp.float32), precision=lax.Precision.HIGHEST).astype(jnp.bfloat16)
    attention = jnp.dot(head_values.reshape(TOKENS, H * VH), out_proj, preferred_element_type=jnp.float32)
    mixed_in = lax.optimization_barrier((residual.astype(jnp.float32) + attention).astype(jnp.bfloat16))
    wide = mixed_in.astype(jnp.float32)
    scale = lax.rsqrt(lax.optimization_barrier(jnp.mean(wide * wide, axis=1, keepdims=True)) + NORM_EPS)
    normed = (wide * scale * norm_gain.astype(jnp.float32)[None, :]).astype(jnp.bfloat16)
    groups = TOKENS // TOK_GRP
    route_groups = routes.reshape(groups, TOK_GRP, TOP)
    labels = jnp.arange(EXPERTS, dtype=jnp.int32)
    chosen = (route_groups[..., None] == labels[None, None, None, :]).astype(jnp.int32)
    routed = lax.optimization_barrier(jnp.sum(chosen, axis=2)).astype(jnp.int32)
    earlier = (jnp.cumsum(routed, axis=1) - routed).astype(jnp.int32)
    slot_ids = jnp.arange(CAP, dtype=jnp.int32)
    routed_t = jnp.transpose(routed, (2, 0, 1))
    earlier_t = jnp.transpose(earlier, (2, 0, 1))
    table = (routed_t[:, :, None, :] > 0) & (earlier_t[:, :, None, :] == slot_ids[None, None, :, None])
    normed_groups = normed.reshape(groups, TOK_GRP, D).astype(jnp.float32)
    tenant_groups = tenant_ids.reshape(groups, TOK_GRP).astype(jnp.int32)
    tenant_labels = jnp.arange(TEN, dtype=jnp.int32)

    def run_expert(inputs):
        choose, gate_w, up_w, down_w, left_w, right_w = inputs
        input_rows = jnp.einsum('ncg,ngd->ncd', choose.astype(jnp.float32), normed_groups, precision=lax.Precision.HIGHEST)
        input_rows = input_rows.astype(jnp.bfloat16).reshape(groups * CAP, D)
        owners = lax.optimization_barrier(jnp.sum(choose.astype(jnp.int32) * tenant_groups[:, None, :], axis=2)).astype(jnp.int32).reshape(groups * CAP)
        gate_scores = jnp.dot(input_rows, gate_w, preferred_element_type=jnp.float32)
        upper_bound = jnp.dot(input_rows, up_w, preferred_element_type=jnp.float32)
        hidden = (jax.nn.silu(gate_scores) * upper_bound).astype(jnp.bfloat16)
        base_output = jnp.dot(hidden, down_w, preferred_element_type=jnp.float32)
        owner_mask = (owners[:, None] == tenant_labels[None, :]).astype(jnp.float32)
        mixing_coefficient = jnp.einsum('sf,tfr->str', hidden.astype(jnp.float32), left_w.astype(jnp.float32), precision=lax.Precision.HIGHEST)
        mixing_coefficient = mixing_coefficient * owner_mask[:, :, None]
        delta = jnp.einsum('str,trd->sd', mixing_coefficient, right_w.astype(jnp.float32), precision=lax.Precision.HIGHEST)
        return (base_output - delta).astype(jnp.bfloat16).reshape(groups, CAP, D)
    outputs = lax.map(run_expert, (table, expert_gate_weight, expert_up_weight, expert_down_weight, jnp.transpose(left_delta_factor, (1, 0, 2, 3)), jnp.transpose(factor_right, (1, 0, 2, 3))))
    gate_of = lax.optimization_barrier(jnp.sum(gate_values.reshape(groups, TOK_GRP, TOP)[..., None] * chosen.astype(jnp.float32), axis=2))
    weighting = table.astype(jnp.float32) * jnp.transpose(gate_of, (2, 0, 1))[:, :, None, :]
    expert_part = jnp.einsum('encg,encd->ngd', weighting, outputs.astype(jnp.float32), precision=lax.Precision.HIGHEST)
    return (wide + expert_part.reshape(TOKENS, D)).astype(jnp.bfloat16)
```

```python
import jax
import jax.numpy as jnp
from jax import lax
from jax.sharding import PartitionSpec as P

LAT = 512
EXPERTS = 16
TEN = 3


SCORE_SCALE = 0.07216878364870323
NORM_EPS = 1e-06
MASKED = -1e30
RT = ("role", "tensor")


def rms_rows(input_rows, norm_gain):
    wide = input_rows.astype(jnp.float32)
    scale = lax.rsqrt(jnp.mean(wide * wide, axis=-1, keepdims=True) + NORM_EPS)
    return (wide * scale * norm_gain.astype(jnp.float32)).astype(jnp.bfloat16)


def slot_table(routes, expert, capacity):
    hit = jnp.any(routes == expert, axis=-1).astype(jnp.int32)
    earlier = jnp.cumsum(hit, axis=-1) - hit
    slot_ids = jnp.arange(capacity, dtype=jnp.int32)
    return (hit[..., None, :] > 0) & (earlier[..., None, :] == slot_ids[:, None])


def local(
    queries,
    latent_cache,
    new_latent,
    cache_lengths,
    value_proj,
    out_proj,
    residual,
    norm_gain,
    routes,
    gate_values,
    tenant_ids,
    expert_gate_weight,
    expert_up_weight,
    expert_down_weight,
    left_delta_factor,
    factor_right,
):
    n_slices = lax.axis_size(RT)
    slice_idx = lax.axis_index(RT)
    group_rows = residual.shape[0]
    capacity = 5 * group_rows // 8
    model_width = expert_down_weight.shape[2]
    col_width = model_width // n_slices

    expert = lax.axis_index("dp")
    labels = jnp.arange(EXPERTS, dtype=jnp.int32)
    table = slot_table(routes, labels[:, None, None], capacity)
    slot_owner = jnp.sum(table.astype(jnp.int32) * tenant_ids[None, None, :], axis=2)
    lanes = 128
    all_owners = lax.all_gather(slot_owner.reshape(-1, lanes), RT, axis=0, tiled=True)
    all_owners = all_owners.reshape(n_slices, EXPERTS, capacity)
    owners = lax.dynamic_index_in_dim(all_owners, expert, 1, keepdims=False)
    owners = owners.reshape(n_slices * capacity)
    down_w = expert_down_weight[0].reshape(expert_down_weight.shape[1], n_slices, col_width)
    down_w = lax.all_to_all(down_w, RT, split_axis=1, concat_axis=0, tiled=True)
    down_w = down_w.reshape(-1, col_width)
    left_local = left_delta_factor[:, 0]
    tenants, hidden_slice, rank = left_local.shape
    left_w = lax.all_gather(left_local.reshape(-1, lanes), RT, axis=0, tiled=True)
    left_w = left_w.reshape(n_slices, tenants, hidden_slice, rank)
    left_w = jnp.transpose(left_w, (1, 0, 2, 3)).reshape(tenants, n_slices * hidden_slice, rank)
    right_w = lax.dynamic_slice_in_dim(factor_right[:, 0], slice_idx * col_width, col_width, 2)

    seq_count, context, width = latent_cache.shape
    local_heads = queries.shape[1]
    paired = queries.reshape(seq_count, 2, local_heads, width)
    scores = (
        jnp.einsum("sqhd,spd->sqhp", paired, latent_cache, preferred_element_type=jnp.float32)
        * SCORE_SCALE
    )
    present = jnp.arange(context, dtype=jnp.int32)[None, :] < cache_lengths[:, None]
    scores = jnp.where(present[:, None, None, :], scores, MASKED)
    fresh_keys = new_latent.reshape(seq_count, 2, width)
    fresh = (
        jnp.einsum("sqhd,skd->sqhk", paired, fresh_keys, preferred_element_type=jnp.float32)
        * SCORE_SCALE
    )
    causal = jnp.arange(2)[:, None] >= jnp.arange(2)[None, :]
    fresh = jnp.where(causal[None, :, None, :], fresh, MASKED)
    top = jnp.maximum(jnp.max(scores, axis=3), jnp.max(fresh, axis=3))[..., None]
    weights = jnp.exp(scores - top)
    fresh_weights = jnp.exp(fresh - top)
    total = jnp.sum(weights, axis=3) + jnp.sum(fresh_weights, axis=3)
    summed = jnp.einsum(
        "sqhp,spd->sqhd",
        weights.astype(jnp.bfloat16),
        latent_cache[:, :, :LAT],
        preferred_element_type=jnp.float32,
    )
    summed = summed + jnp.einsum(
        "sqhk,skd->sqhd",
        fresh_weights.astype(jnp.bfloat16),
        fresh_keys[:, :, :LAT],
        preferred_element_type=jnp.float32,
    )
    attended = (
        (summed / total[..., None]).astype(jnp.bfloat16).reshape(seq_count * 2, local_heads, LAT)
    )
    by_head = lax.all_to_all(attended, "tensor", split_axis=1, concat_axis=0, tiled=True)
    head_values = jnp.einsum(
        "thl,hlv->thv", by_head, value_proj, preferred_element_type=jnp.float32
    ).astype(jnp.bfloat16)
    head_values = head_values.reshape(
        head_values.shape[0], head_values.shape[1] * head_values.shape[2]
    )
    all_values = lax.all_gather(head_values, "dp", axis=0, tiled=True)
    attention = lax.psum_scatter(
        jnp.dot(all_values, out_proj, preferred_element_type=jnp.float32),
        RT,
        scatter_dimension=0,
        tiled=True,
    )
    mixed_in = lax.optimization_barrier(
        (residual.astype(jnp.float32) + attention).astype(jnp.bfloat16)
    )

    full_rows = lax.all_gather(mixed_in.reshape(-1, lanes), "dp", axis=0, tiled=True)
    full_rows = full_rows.reshape(-1, group_rows, mixed_in.shape[1])
    full_rows = jnp.transpose(full_rows, (1, 0, 2)).reshape(group_rows, model_width)
    normed = rms_rows(full_rows, norm_gain)
    mine = lax.dynamic_index_in_dim(table, expert, 0, keepdims=False)
    picked = jnp.dot(
        mine.astype(jnp.bfloat16), normed, preferred_element_type=jnp.float32
    ).astype(jnp.bfloat16)
    collected_rows = lax.all_gather(picked, RT, axis=0, tiled=True)
    gate_scores = jnp.dot(collected_rows, expert_gate_weight[0], preferred_element_type=jnp.float32)
    upper_bound = jnp.dot(collected_rows, expert_up_weight[0], preferred_element_type=jnp.float32)
    hidden = (jax.nn.silu(gate_scores) * upper_bound).astype(jnp.bfloat16)

    hidden_all = lax.all_gather(hidden, RT, axis=0, tiled=False)
    hidden_all = jnp.transpose(hidden_all, (1, 0, 2)).reshape(hidden.shape[0], -1)
    base_output = jnp.dot(hidden_all, down_w, preferred_element_type=jnp.float32)
    owner_mask = (owners[:, None] == jnp.arange(TEN, dtype=jnp.int32)[None, :]).astype(jnp.float32)
    mixing = jnp.einsum(
        "sf,tfr->str", hidden_all, left_w, preferred_element_type=jnp.float32
    ) * owner_mask[:, :, None]
    delta = jnp.einsum(
        "str,trd->sd", mixing, right_w.astype(jnp.float32), precision=lax.Precision.HIGHEST
    )
    expert_out = (base_output - delta).astype(jnp.bfloat16)
    expert_out = expert_out.reshape(n_slices, capacity, col_width)
    by_group = lax.all_to_all(expert_out, RT, split_axis=0, concat_axis=0, tiled=True)
    by_expert = lax.all_to_all(by_group, "dp", split_axis=0, concat_axis=0, tiled=True)

    chosen = (routes[:, :, None] == labels[None, None, :]).astype(jnp.float32)
    gate_of = jnp.sum(gate_values[:, :, None] * chosen, axis=1)
    weighting = table.astype(jnp.float32) * gate_of.T[:, None, :]
    expert_part = jnp.einsum(
        "ecg,ecd->gd", weighting, by_expert.astype(jnp.float32), precision=lax.Precision.HIGHEST
    )
    return (mixed_in.astype(jnp.float32) + expert_part).astype(jnp.bfloat16)


def solution(mesh):
    placed = (
        P(("dp", "tensor"), "role", None),
        P(("dp", "tensor"), None, None),
        P(("dp", "tensor"), None),
        P(("dp", "tensor")),
        P(("role", "tensor"), None, None),
        P(("role", "tensor"), "dp"),
        P(("role", "tensor"), "dp"),
        P(),
        P(("role", "tensor"), None),
        P(("role", "tensor"), None),
        P(("role", "tensor")),
        P("dp", None, ("role", "tensor")),
        P("dp", None, ("role", "tensor")),
        P("dp", ("role", "tensor"), None),
        P(None, "dp", ("role", "tensor"), None),
        P(None, "dp", None, None),
    )
    return jax.shard_map(
        local, mesh=mesh, in_specs=placed, out_specs=P(("role", "tensor"), "dp"), check_vma=False
    )
```

```python
import jax
import jax.numpy as jnp
from jax import lax
from jax.sharding import PartitionSpec as P

LAT = 512
EXPERTS = 16
TEN = 3


SCORE_SCALE = 0.07216878364870323
NORM_EPS = 1e-06
MASKED = -1e30
RT = ("role", "tensor")


def rms_rows(input_rows, norm_gain):
    wide = input_rows.astype(jnp.float32)
    scale = lax.rsqrt(jnp.mean(wide * wide, axis=-1, keepdims=True) + NORM_EPS)
    return (wide * scale * norm_gain.astype(jnp.float32)).astype(jnp.bfloat16)


def slot_table(routes, expert, capacity):
    hit = jnp.any(routes == expert, axis=-1).astype(jnp.int32)
    earlier = jnp.cumsum(hit, axis=-1) - hit
    slot_ids = jnp.arange(capacity, dtype=jnp.int32)
    return (hit[..., None, :] > 0) & (earlier[..., None, :] == slot_ids[:, None])


def local(
    queries,
    latent_cache,
    new_latent,
    cache_lengths,
    value_proj,
    out_proj,
    residual,
    norm_gain,
    routes,
    gate_values,
    tenant_ids,
    expert_gate_weight,
    expert_up_weight,
    expert_down_weight,
    left_delta_factor,
    factor_right,
):
    n_slices = lax.axis_size(RT)
    slice_idx = lax.axis_index(RT)
    group_rows = residual.shape[0]
    capacity = 5 * group_rows // 8
    model_width = expert_down_weight.shape[2]
    col_width = model_width // n_slices

    expert = lax.axis_index("dp")
    labels = jnp.arange(EXPERTS, dtype=jnp.int32)
    table = slot_table(routes, labels[:, None, None], capacity)
    mine = lax.dynamic_index_in_dim(table, expert, 0, keepdims=False)
    mine_owner = jnp.sum(mine.astype(jnp.int32) * tenant_ids[None, :], axis=1)
    hidden_slice = expert_down_weight.shape[1]
    down_local = expert_down_weight[0].reshape(hidden_slice, n_slices, col_width)
    left_local = left_delta_factor[:, 0]
    tenants, _, rank = left_local.shape
    left_local = jnp.transpose(left_local, (1, 0, 2)).reshape(hidden_slice, 1, tenants * rank)
    left_local = jnp.broadcast_to(left_local, (hidden_slice, n_slices, tenants * rank))
    down_pack = jnp.concatenate([down_local, left_local], axis=2)
    down_pack = lax.all_to_all(down_pack, RT, split_axis=1, concat_axis=0, tiled=True)
    right_w = lax.dynamic_slice_in_dim(factor_right[:, 0], slice_idx * col_width, col_width, 2)

    seq_count, context, width = latent_cache.shape
    local_heads = queries.shape[1]
    paired = queries.reshape(seq_count, 2, local_heads, width)
    scores = (
        jnp.einsum("sqhd,spd->sqhp", paired, latent_cache, preferred_element_type=jnp.float32)
        * SCORE_SCALE
    )
    present = jnp.arange(context, dtype=jnp.int32)[None, :] < cache_lengths[:, None]
    scores = jnp.where(present[:, None, None, :], scores, MASKED)
    fresh_keys = new_latent.reshape(seq_count, 2, width)
    fresh = (
        jnp.einsum("sqhd,skd->sqhk", paired, fresh_keys, preferred_element_type=jnp.float32)
        * SCORE_SCALE
    )
    causal = jnp.arange(2)[:, None] >= jnp.arange(2)[None, :]
    fresh = jnp.where(causal[None, :, None, :], fresh, MASKED)
    top = jnp.maximum(jnp.max(scores, axis=3), jnp.max(fresh, axis=3))[..., None]
    weights = jnp.exp(scores - top)
    fresh_weights = jnp.exp(fresh - top)
    total = jnp.sum(weights, axis=3) + jnp.sum(fresh_weights, axis=3)
    summed = jnp.einsum(
        "sqhp,spd->sqhd",
        weights.astype(jnp.bfloat16),
        latent_cache[:, :, :LAT],
        preferred_element_type=jnp.float32,
    )
    summed = summed + jnp.einsum(
        "sqhk,skd->sqhd",
        fresh_weights.astype(jnp.bfloat16),
        fresh_keys[:, :, :LAT],
        preferred_element_type=jnp.float32,
    )
    attended = (
        (summed / total[..., None]).astype(jnp.bfloat16).reshape(seq_count * 2, local_heads, LAT)
    )
    by_head = lax.all_to_all(attended, "tensor", split_axis=1, concat_axis=0, tiled=True)
    head_values = jnp.einsum(
        "thl,hlv->thv", by_head, value_proj, preferred_element_type=jnp.float32
    ).astype(jnp.bfloat16)
    head_values = head_values.reshape(
        head_values.shape[0], head_values.shape[1] * head_values.shape[2]
    )
    all_values = lax.all_gather(head_values, "dp", axis=0, tiled=True)
    down_pack, all_values = lax.optimization_barrier((down_pack, all_values))
    partial = jnp.dot(all_values, out_proj, preferred_element_type=jnp.float32)
    partial = lax.psum_scatter(partial, "role", scatter_dimension=0, tiled=True)
    attention = lax.psum_scatter(partial, "tensor", scatter_dimension=0, tiled=True)
    mixed_in = lax.optimization_barrier(
        (residual.astype(jnp.float32) + attention).astype(jnp.bfloat16)
    )

    full_rows = lax.all_gather(mixed_in.reshape(-1, 128), "dp", axis=0, tiled=True)
    full_rows = full_rows.reshape(-1, group_rows, mixed_in.shape[1])
    full_rows = jnp.transpose(full_rows, (1, 0, 2)).reshape(group_rows, model_width)
    normed = rms_rows(full_rows, norm_gain)
    picked = jnp.dot(
        mine.astype(jnp.bfloat16), normed, preferred_element_type=jnp.float32
    ).astype(jnp.bfloat16)
    collected_rows = lax.all_gather(picked, RT, axis=0, tiled=True)
    gate_scores = jnp.dot(collected_rows, expert_gate_weight[0], preferred_element_type=jnp.float32)
    upper_bound = jnp.dot(collected_rows, expert_up_weight[0], preferred_element_type=jnp.float32)
    hidden = (jax.nn.silu(gate_scores) * upper_bound).astype(jnp.bfloat16)

    lanes = hidden.shape[1]
    owner_block = jnp.zeros((8, lanes), jnp.bfloat16)
    owner_block = owner_block.at[0, :capacity].set(mine_owner.astype(jnp.bfloat16))
    hidden_ext = jnp.concatenate([hidden, owner_block], axis=0)
    gathered = lax.all_gather(hidden_ext, RT, axis=0, tiled=True)
    gathered = gathered.reshape(n_slices, hidden.shape[0] + 8, lanes)
    owners = gathered[:, hidden.shape[0], :capacity].astype(jnp.int32).reshape(n_slices * capacity)
    hidden_all = jnp.transpose(gathered[:, : hidden.shape[0]], (1, 0, 2)).reshape(hidden.shape[0], -1)
    down_pack = down_pack.reshape(n_slices * hidden_slice, col_width + tenants * rank)
    down_w = down_pack[:, :col_width]
    left_w = down_pack[:, col_width:].reshape(n_slices * hidden_slice, tenants, rank)
    base_output = jnp.dot(hidden_all, down_w, preferred_element_type=jnp.float32)
    owner_mask = (owners[:, None] == jnp.arange(TEN, dtype=jnp.int32)[None, :]).astype(jnp.float32)
    mixing = jnp.einsum(
        "sf,ftr->str", hidden_all, left_w, preferred_element_type=jnp.float32
    ) * owner_mask[:, :, None]
    delta = jnp.einsum(
        "str,trd->sd", mixing, right_w.astype(jnp.float32), precision=lax.Precision.HIGHEST
    )
    expert_out = (base_output - delta).astype(jnp.bfloat16)
    expert_out = expert_out.reshape(n_slices, capacity, col_width)
    by_group = lax.all_to_all(expert_out, RT, split_axis=0, concat_axis=0, tiled=True)
    by_expert = lax.all_to_all(by_group, "dp", split_axis=0, concat_axis=0, tiled=True)

    chosen = (routes[:, :, None] == labels[None, None, :]).astype(jnp.float32)
    gate_of = jnp.sum(gate_values[:, :, None] * chosen, axis=1)
    weighting = table.astype(jnp.float32) * gate_of.T[:, None, :]
    expert_part = jnp.einsum(
        "ecg,ecd->gd", weighting, by_expert.astype(jnp.float32), precision=lax.Precision.HIGHEST
    )
    return (mixed_in.astype(jnp.float32) + expert_part).astype(jnp.bfloat16)


def solution(mesh):
    placed = (
        P(("dp", "tensor"), "role", None),
        P(("dp", "tensor"), None, None),
        P(("dp", "tensor"), None),
        P(("dp", "tensor")),
        P(("role", "tensor"), None, None),
        P(("role", "tensor"), "dp"),
        P(("role", "tensor"), "dp"),
        P(),
        P(("role", "tensor"), None),
        P(("role", "tensor"), None),
        P(("role", "tensor")),
        P("dp", None, ("role", "tensor")),
        P("dp", None, ("role", "tensor")),
        P("dp", ("role", "tensor"), None),
        P(None, "dp", ("role", "tensor"), None),
        P(None, "dp", None, None),
    )
    return jax.shard_map(
        local, mesh=mesh, in_specs=placed, out_specs=P(("role", "tensor"), "dp"), check_vma=False
    )
```

```python
import jax
import jax.numpy as jnp
from jax import lax
from jax.sharding import PartitionSpec as P

LAT = 512
EXPERTS = 16
TEN = 3


SCORE_SCALE = 0.07216878364870323
NORM_EPS = 1e-06
MASKED = -1e30
RT = ("role", "tensor")


def rms_rows(input_rows, norm_gain):
    wide = input_rows.astype(jnp.float32)
    scale = lax.rsqrt(jnp.mean(wide * wide, axis=-1, keepdims=True) + NORM_EPS)
    return (wide * scale * norm_gain.astype(jnp.float32)).astype(jnp.bfloat16)


def slot_table(routes, expert, capacity):
    hit = jnp.any(routes == expert, axis=-1).astype(jnp.int32)
    earlier = jnp.cumsum(hit, axis=-1) - hit
    slot_ids = jnp.arange(capacity, dtype=jnp.int32)
    return (hit[..., None, :] > 0) & (earlier[..., None, :] == slot_ids[:, None])


def local(
    queries,
    latent_cache,
    new_latent,
    cache_lengths,
    value_proj,
    out_proj,
    residual,
    norm_gain,
    routes,
    gate_values,
    tenant_ids,
    expert_gate_weight,
    expert_up_weight,
    expert_down_weight,
    left_delta_factor,
    factor_right,
):
    n_slices = lax.axis_size(RT)
    slice_idx = lax.axis_index(RT)
    group_rows = residual.shape[0]
    capacity = 5 * group_rows // 8
    model_width = expert_down_weight.shape[2]
    col_width = model_width // n_slices

    expert = lax.axis_index("dp")
    labels = jnp.arange(EXPERTS, dtype=jnp.int32)
    table = slot_table(routes, labels[:, None, None], capacity)
    mine = lax.dynamic_index_in_dim(table, expert, 0, keepdims=False)
    mine_owner = jnp.sum(mine.astype(jnp.int32) * tenant_ids[None, :], axis=1)
    hidden_slice = expert_down_weight.shape[1]
    down_local = expert_down_weight[0].reshape(hidden_slice, n_slices, col_width)
    left_local = left_delta_factor[:, 0]
    tenants, _, rank = left_local.shape
    left_local = jnp.transpose(left_local, (1, 0, 2)).reshape(hidden_slice, 1, tenants * rank)
    left_local = jnp.broadcast_to(left_local, (hidden_slice, n_slices, tenants * rank))
    down_pack = jnp.concatenate([down_local, left_local], axis=2)
    pack_width = down_pack.shape[2]
    slot_token = jnp.sum(mine.astype(jnp.int32) * jnp.arange(group_rows, dtype=jnp.int32)[None, :], axis=1)
    slot_used = jnp.sum(mine.astype(jnp.int32), axis=1)
    info = jnp.concatenate([slot_token, slot_used, mine_owner]).astype(jnp.bfloat16)
    info_rows = jnp.zeros((8, pack_width), jnp.bfloat16).at[0, : info.shape[0]].set(info)
    info_rows = jnp.broadcast_to(info_rows[:, None, :], (8, n_slices, pack_width))
    down_pack = jnp.concatenate([down_pack, info_rows], axis=0)
    down_pack = lax.all_to_all(down_pack, RT, split_axis=1, concat_axis=0, tiled=True)
    right_w = lax.dynamic_slice_in_dim(factor_right[:, 0], slice_idx * col_width, col_width, 2)

    seq_count, context, width = latent_cache.shape
    local_heads = queries.shape[1]
    paired = queries.reshape(seq_count, 2, local_heads, width)
    scores = (
        jnp.einsum("sqhd,spd->sqhp", paired, latent_cache, preferred_element_type=jnp.float32)
        * SCORE_SCALE
    )
    present = jnp.arange(context, dtype=jnp.int32)[None, :] < cache_lengths[:, None]
    scores = jnp.where(present[:, None, None, :], scores, MASKED)
    fresh_keys = new_latent.reshape(seq_count, 2, width)
    fresh = (
        jnp.einsum("sqhd,skd->sqhk", paired, fresh_keys, preferred_element_type=jnp.float32)
        * SCORE_SCALE
    )
    causal = jnp.arange(2)[:, None] >= jnp.arange(2)[None, :]
    fresh = jnp.where(causal[None, :, None, :], fresh, MASKED)
    top = jnp.maximum(jnp.max(scores, axis=3), jnp.max(fresh, axis=3))[..., None]
    weights = jnp.exp(scores - top)
    fresh_weights = jnp.exp(fresh - top)
    total = jnp.sum(weights, axis=3) + jnp.sum(fresh_weights, axis=3)
    summed = jnp.einsum(
        "sqhp,spd->sqhd",
        weights.astype(jnp.bfloat16),
        latent_cache[:, :, :LAT],
        preferred_element_type=jnp.float32,
    )
    summed = summed + jnp.einsum(
        "sqhk,skd->sqhd",
        fresh_weights.astype(jnp.bfloat16),
        fresh_keys[:, :, :LAT],
        preferred_element_type=jnp.float32,
    )
    attended = (
        (summed / total[..., None]).astype(jnp.bfloat16).reshape(seq_count * 2, local_heads, LAT)
    )
    by_head = lax.all_to_all(attended, "tensor", split_axis=1, concat_axis=0, tiled=True)
    head_values = jnp.einsum(
        "thl,hlv->thv", by_head, value_proj, preferred_element_type=jnp.float32
    ).astype(jnp.bfloat16)
    head_values = head_values.reshape(
        head_values.shape[0], head_values.shape[1] * head_values.shape[2]
    )
    all_values = lax.all_gather(head_values, "dp", axis=0, tiled=True)
    down_pack, all_values = lax.optimization_barrier((down_pack, all_values))
    partial = jnp.dot(all_values, out_proj, preferred_element_type=jnp.float32)
    partial = lax.psum_scatter(partial, "role", scatter_dimension=0, tiled=True)
    attention = lax.psum_scatter(partial, "tensor", scatter_dimension=0, tiled=True)
    mixed_in = lax.optimization_barrier(
        (residual.astype(jnp.float32) + attention).astype(jnp.bfloat16)
    )

    down_pack = down_pack.reshape(n_slices, hidden_slice + 8, pack_width)
    info = down_pack[:, hidden_slice, : 3 * capacity].astype(jnp.int32)
    slot_token, slot_used, owners = info[:, :capacity], info[:, capacity : 2 * capacity], info[:, 2 * capacity :]
    owners = owners.reshape(n_slices * capacity)
    n_cols = lax.axis_size("dp")
    everything = lax.all_gather(mixed_in, ("role", "tensor", "dp"), axis=0, tiled=True)
    everything = everything.reshape(n_slices, n_cols, group_rows, mixed_in.shape[1])
    one_hot = (slot_token[:, :, None] == jnp.arange(group_rows, dtype=jnp.int32)[None, None, :]) & (
        slot_used[:, :, None] > 0
    )
    picked = jnp.einsum(
        "ncg,ndgk->ncdk", one_hot.astype(jnp.bfloat16), everything, preferred_element_type=jnp.float32
    )
    picked = picked.reshape(n_slices * capacity, model_width)
    scale = lax.rsqrt(jnp.mean(picked * picked, axis=-1, keepdims=True) + NORM_EPS)
    collected_rows = (picked * scale * norm_gain.astype(jnp.float32)).astype(jnp.bfloat16)
    gate_scores = jnp.dot(collected_rows, expert_gate_weight[0], preferred_element_type=jnp.float32)
    upper_bound = jnp.dot(collected_rows, expert_up_weight[0], preferred_element_type=jnp.float32)
    hidden = (jax.nn.silu(gate_scores) * upper_bound).astype(jnp.bfloat16)

    gathered = lax.all_gather(hidden, RT, axis=0, tiled=False)
    hidden_all = jnp.transpose(gathered, (1, 0, 2)).reshape(hidden.shape[0], -1)
    down_pack = down_pack[:, :hidden_slice].reshape(n_slices * hidden_slice, pack_width)
    down_w = down_pack[:, :col_width]
    left_w = down_pack[:, col_width:].reshape(n_slices * hidden_slice, tenants, rank)
    base_output = jnp.dot(hidden_all, down_w, preferred_element_type=jnp.float32)
    owner_mask = (owners[:, None] == jnp.arange(TEN, dtype=jnp.int32)[None, :]).astype(jnp.float32)
    mixing = jnp.einsum(
        "sf,ftr->str", hidden_all, left_w, preferred_element_type=jnp.float32
    ) * owner_mask[:, :, None]
    delta = jnp.einsum(
        "str,trd->sd", mixing, right_w.astype(jnp.float32), precision=lax.Precision.HIGHEST
    )
    expert_out = (base_output - delta).astype(jnp.bfloat16)
    expert_out = expert_out.reshape(n_slices, capacity, col_width)
    by_group = lax.all_to_all(expert_out, RT, split_axis=0, concat_axis=0, tiled=True)
    by_expert = lax.all_to_all(by_group, "dp", split_axis=0, concat_axis=0, tiled=True)

    chosen = (routes[:, :, None] == labels[None, None, :]).astype(jnp.float32)
    gate_of = jnp.sum(gate_values[:, :, None] * chosen, axis=1)
    weighting = table.astype(jnp.float32) * gate_of.T[:, None, :]
    expert_part = jnp.einsum(
        "ecg,ecd->gd", weighting, by_expert.astype(jnp.float32), precision=lax.Precision.HIGHEST
    )
    return (mixed_in.astype(jnp.float32) + expert_part).astype(jnp.bfloat16)


def solution(mesh):
    placed = (
        P(("dp", "tensor"), "role", None),
        P(("dp", "tensor"), None, None),
        P(("dp", "tensor"), None),
        P(("dp", "tensor")),
        P(("role", "tensor"), None, None),
        P(("role", "tensor"), "dp"),
        P(("role", "tensor"), "dp"),
        P(),
        P(("role", "tensor"), None),
        P(("role", "tensor"), None),
        P(("role", "tensor")),
        P("dp", None, ("role", "tensor")),
        P("dp", None, ("role", "tensor")),
        P("dp", ("role", "tensor"), None),
        P(None, "dp", ("role", "tensor"), None),
        P(None, "dp", None, None),
    )
    return jax.shard_map(
        local, mesh=mesh, in_specs=placed, out_specs=P(("role", "tensor"), "dp"), check_vma=False
    )
```

```python
import jax
import jax.numpy as jnp
from jax import lax
from jax.sharding import PartitionSpec as P

LAT = 512
EXPERTS = 16
TEN = 3


SCORE_SCALE = 0.07216878364870323
NORM_EPS = 1e-06
MASKED = -1e30
RT = ("role", "tensor")


def rms_rows(input_rows, norm_gain):
    wide = input_rows.astype(jnp.float32)
    scale = lax.rsqrt(jnp.mean(wide * wide, axis=-1, keepdims=True) + NORM_EPS)
    return (wide * scale * norm_gain.astype(jnp.float32)).astype(jnp.bfloat16)


def slot_table(routes, expert, capacity):
    hit = jnp.any(routes == expert, axis=-1).astype(jnp.int32)
    earlier = jnp.cumsum(hit, axis=-1) - hit
    slot_ids = jnp.arange(capacity, dtype=jnp.int32)
    return (hit[..., None, :] > 0) & (earlier[..., None, :] == slot_ids[:, None])


def local(
    queries,
    latent_cache,
    new_latent,
    cache_lengths,
    value_proj,
    out_proj,
    residual,
    norm_gain,
    routes,
    gate_values,
    tenant_ids,
    expert_gate_weight,
    expert_up_weight,
    expert_down_weight,
    left_delta_factor,
    factor_right,
):
    n_slices = lax.axis_size(RT)
    slice_idx = lax.axis_index(RT)
    group_rows = residual.shape[0]
    capacity = 5 * group_rows // 8
    model_width = expert_down_weight.shape[2]
    col_width = model_width // n_slices

    expert = lax.axis_index("dp")
    labels = jnp.arange(EXPERTS, dtype=jnp.int32)
    table = slot_table(routes, labels[:, None, None], capacity)
    mine = lax.dynamic_index_in_dim(table, expert, 0, keepdims=False)
    mine_owner = jnp.sum(mine.astype(jnp.int32) * tenant_ids[None, :], axis=1)
    hidden_slice = expert_down_weight.shape[1]
    down_local = expert_down_weight[0].reshape(hidden_slice, n_slices, col_width)
    left_local = left_delta_factor[:, 0]
    tenants, _, rank = left_local.shape
    left_local = jnp.transpose(left_local, (1, 0, 2)).reshape(hidden_slice, 1, tenants * rank)
    left_local = jnp.broadcast_to(left_local, (hidden_slice, n_slices, tenants * rank))
    down_pack = jnp.concatenate([down_local, left_local], axis=2)
    down_pack = lax.all_to_all(down_pack, RT, split_axis=1, concat_axis=0, tiled=True)
    right_w = lax.dynamic_slice_in_dim(factor_right[:, 0], slice_idx * col_width, col_width, 2)

    seq_count, context, width = latent_cache.shape
    local_heads = queries.shape[1]
    paired = queries.reshape(seq_count, 2, local_heads, width)
    scores = (
        jnp.einsum("sqhd,spd->sqhp", paired, latent_cache, preferred_element_type=jnp.float32)
        * SCORE_SCALE
    )
    present = jnp.arange(context, dtype=jnp.int32)[None, :] < cache_lengths[:, None]
    scores = jnp.where(present[:, None, None, :], scores, MASKED)
    fresh_keys = new_latent.reshape(seq_count, 2, width)
    fresh = (
        jnp.einsum("sqhd,skd->sqhk", paired, fresh_keys, preferred_element_type=jnp.float32)
        * SCORE_SCALE
    )
    causal = jnp.arange(2)[:, None] >= jnp.arange(2)[None, :]
    fresh = jnp.where(causal[None, :, None, :], fresh, MASKED)
    top = jnp.maximum(jnp.max(scores, axis=3), jnp.max(fresh, axis=3))[..., None]
    weights = jnp.exp(scores - top)
    fresh_weights = jnp.exp(fresh - top)
    total = jnp.sum(weights, axis=3) + jnp.sum(fresh_weights, axis=3)
    summed = jnp.einsum(
        "sqhp,spd->sqhd",
        weights.astype(jnp.bfloat16),
        latent_cache[:, :, :LAT],
        preferred_element_type=jnp.float32,
    )
    summed = summed + jnp.einsum(
        "sqhk,skd->sqhd",
        fresh_weights.astype(jnp.bfloat16),
        fresh_keys[:, :, :LAT],
        preferred_element_type=jnp.float32,
    )
    attended = (
        (summed / total[..., None]).astype(jnp.bfloat16).reshape(seq_count * 2, local_heads, LAT)
    )
    by_head = lax.all_to_all(attended, "tensor", split_axis=1, concat_axis=0, tiled=True)
    head_values = jnp.einsum(
        "thl,hlv->thv", by_head, value_proj, preferred_element_type=jnp.float32
    ).astype(jnp.bfloat16)
    head_values = head_values.reshape(
        head_values.shape[0], head_values.shape[1] * head_values.shape[2]
    )
    all_values = lax.all_gather(head_values, "dp", axis=0, tiled=True)
    down_pack, all_values = lax.optimization_barrier((down_pack, all_values))
    partial = jnp.dot(all_values, out_proj, preferred_element_type=jnp.float32)
    half = partial.shape[0] // 2
    role_idx = lax.axis_index("role")
    keep = lax.dynamic_slice_in_dim(partial, role_idx * half, half, 0)
    give = lax.dynamic_slice_in_dim(partial, (1 - role_idx) * half, half, 0)
    partial = keep + lax.ppermute(give, "role", [(0, 1), (1, 0)])
    attention = lax.psum_scatter(partial, "tensor", scatter_dimension=0, tiled=True)
    mixed_in = lax.optimization_barrier(
        (residual.astype(jnp.float32) + attention).astype(jnp.bfloat16)
    )

    full_rows = lax.all_gather(mixed_in.reshape(-1, 128), "dp", axis=0, tiled=True)
    full_rows = full_rows.reshape(-1, group_rows, mixed_in.shape[1])
    full_rows = jnp.transpose(full_rows, (1, 0, 2)).reshape(group_rows, model_width)
    normed = rms_rows(full_rows, norm_gain)
    picked = jnp.dot(
        mine.astype(jnp.bfloat16), normed, preferred_element_type=jnp.float32
    ).astype(jnp.bfloat16)
    collected_rows = lax.all_gather(picked, RT, axis=0, tiled=True)
    gate_scores = jnp.dot(collected_rows, expert_gate_weight[0], preferred_element_type=jnp.float32)
    upper_bound = jnp.dot(collected_rows, expert_up_weight[0], preferred_element_type=jnp.float32)
    hidden = (jax.nn.silu(gate_scores) * upper_bound).astype(jnp.bfloat16)

    lanes = hidden.shape[1]
    owner_block = jnp.zeros((8, lanes), jnp.bfloat16)
    owner_block = owner_block.at[0, :capacity].set(mine_owner.astype(jnp.bfloat16))
    hidden_ext = jnp.concatenate([hidden, owner_block], axis=0)
    gathered = lax.all_gather(hidden_ext, RT, axis=0, tiled=True)
    gathered = gathered.reshape(n_slices, hidden.shape[0] + 8, lanes)
    owners = gathered[:, hidden.shape[0], :capacity].astype(jnp.int32).reshape(n_slices * capacity)
    hidden_all = jnp.transpose(gathered[:, : hidden.shape[0]], (1, 0, 2)).reshape(hidden.shape[0], -1)
    down_pack = down_pack.reshape(n_slices * hidden_slice, col_width + tenants * rank)
    down_w = down_pack[:, :col_width]
    left_w = down_pack[:, col_width:].reshape(n_slices * hidden_slice, tenants, rank)
    base_output = jnp.dot(hidden_all, down_w, preferred_element_type=jnp.float32)
    owner_mask = (owners[:, None] == jnp.arange(TEN, dtype=jnp.int32)[None, :]).astype(jnp.float32)
    mixing = jnp.einsum(
        "sf,ftr->str", hidden_all, left_w, preferred_element_type=jnp.float32
    ) * owner_mask[:, :, None]
    delta = jnp.einsum(
        "str,trd->sd", mixing, right_w.astype(jnp.float32), precision=lax.Precision.HIGHEST
    )
    expert_out = (base_output - delta).astype(jnp.bfloat16)
    expert_out = expert_out.reshape(n_slices, capacity, col_width)
    by_group = lax.all_to_all(expert_out, RT, split_axis=0, concat_axis=0, tiled=True)
    by_expert = lax.all_to_all(by_group, "dp", split_axis=0, concat_axis=0, tiled=True)

    chosen = (routes[:, :, None] == labels[None, None, :]).astype(jnp.float32)
    gate_of = jnp.sum(gate_values[:, :, None] * chosen, axis=1)
    weighting = table.astype(jnp.float32) * gate_of.T[:, None, :]
    expert_part = jnp.einsum(
        "ecg,ecd->gd", weighting, by_expert.astype(jnp.float32), precision=lax.Precision.HIGHEST
    )
    return (mixed_in.astype(jnp.float32) + expert_part).astype(jnp.bfloat16)


def solution(mesh):
    placed = (
        P(("dp", "tensor"), "role", None),
        P(("dp", "tensor"), None, None),
        P(("dp", "tensor"), None),
        P(("dp", "tensor")),
        P(("role", "tensor"), None, None),
        P(("role", "tensor"), "dp"),
        P(("role", "tensor"), "dp"),
        P(),
        P(("role", "tensor"), None),
        P(("role", "tensor"), None),
        P(("role", "tensor")),
        P("dp", None, ("role", "tensor")),
        P("dp", None, ("role", "tensor")),
        P("dp", ("role", "tensor"), None),
        P(None, "dp", ("role", "tensor"), None),
        P(None, "dp", None, None),
    )
    return jax.shard_map(
        local, mesh=mesh, in_specs=placed, out_specs=P(("role", "tensor"), "dp"), check_vma=False
    )
```

```python
import jax
import jax.numpy as jnp
from jax import lax
from jax.sharding import PartitionSpec as P

LAT = 512
EXPERTS = 16
TEN = 3


SCORE_SCALE = 0.07216878364870323
NORM_EPS = 1e-06
MASKED = -1e30
RT = ("role", "tensor")


def rms_rows(input_rows, norm_gain):
    wide = input_rows.astype(jnp.float32)
    scale = lax.rsqrt(jnp.mean(wide * wide, axis=-1, keepdims=True) + NORM_EPS)
    return (wide * scale * norm_gain.astype(jnp.float32)).astype(jnp.bfloat16)


def slot_table(routes, expert, capacity):
    hit = jnp.any(routes == expert, axis=-1).astype(jnp.int32)
    earlier = jnp.cumsum(hit, axis=-1) - hit
    slot_ids = jnp.arange(capacity, dtype=jnp.int32)
    return (hit[..., None, :] > 0) & (earlier[..., None, :] == slot_ids[:, None])


def local(
    queries,
    latent_cache,
    new_latent,
    cache_lengths,
    value_proj,
    out_proj,
    residual,
    norm_gain,
    routes,
    gate_values,
    tenant_ids,
    expert_gate_weight,
    expert_up_weight,
    expert_down_weight,
    left_delta_factor,
    factor_right,
):
    n_slices = lax.axis_size(RT)
    slice_idx = lax.axis_index(RT)
    group_rows = residual.shape[0]
    capacity = 5 * group_rows // 8
    model_width = expert_down_weight.shape[2]
    col_width = model_width // n_slices

    expert = lax.axis_index("dp")
    labels = jnp.arange(EXPERTS, dtype=jnp.int32)
    table = slot_table(routes, labels[:, None, None], capacity)
    mine = lax.dynamic_index_in_dim(table, expert, 0, keepdims=False)
    mine_owner = jnp.sum(mine.astype(jnp.int32) * tenant_ids[None, :], axis=1)
    hidden_slice = expert_down_weight.shape[1]
    down_local = expert_down_weight[0].reshape(hidden_slice, n_slices, col_width)
    left_local = left_delta_factor[:, 0]
    tenants, _, rank = left_local.shape
    left_local = jnp.transpose(left_local, (1, 0, 2)).reshape(hidden_slice, 1, tenants * rank)
    left_local = jnp.broadcast_to(left_local, (hidden_slice, n_slices, tenants * rank))
    down_pack = jnp.concatenate([down_local, left_local], axis=2)
    down_pack = lax.all_to_all(down_pack, RT, split_axis=1, concat_axis=0, tiled=True)
    right_w = lax.dynamic_slice_in_dim(factor_right[:, 0], slice_idx * col_width, col_width, 2)

    seq_count, context, width = latent_cache.shape
    local_heads = queries.shape[1]
    paired = queries.reshape(seq_count, 2, local_heads, width)
    scores = (
        jnp.einsum("sqhd,spd->sqhp", paired, latent_cache, preferred_element_type=jnp.float32)
        * SCORE_SCALE
    )
    present = jnp.arange(context, dtype=jnp.int32)[None, :] < cache_lengths[:, None]
    scores = jnp.where(present[:, None, None, :], scores, MASKED)
    fresh_keys = new_latent.reshape(seq_count, 2, width)
    fresh = (
        jnp.einsum("sqhd,skd->sqhk", paired, fresh_keys, preferred_element_type=jnp.float32)
        * SCORE_SCALE
    )
    causal = jnp.arange(2)[:, None] >= jnp.arange(2)[None, :]
    fresh = jnp.where(causal[None, :, None, :], fresh, MASKED)
    top = jnp.maximum(jnp.max(scores, axis=3), jnp.max(fresh, axis=3))[..., None]
    weights = jnp.exp(scores - top)
    fresh_weights = jnp.exp(fresh - top)
    total = jnp.sum(weights, axis=3) + jnp.sum(fresh_weights, axis=3)
    summed = jnp.einsum(
        "sqhp,spd->sqhd",
        weights.astype(jnp.bfloat16),
        latent_cache[:, :, :LAT],
        preferred_element_type=jnp.float32,
    )
    summed = summed + jnp.einsum(
        "sqhk,skd->sqhd",
        fresh_weights.astype(jnp.bfloat16),
        fresh_keys[:, :, :LAT],
        preferred_element_type=jnp.float32,
    )
    attended = (
        (summed / total[..., None]).astype(jnp.bfloat16).reshape(seq_count * 2, local_heads, LAT)
    )
    by_head = lax.all_to_all(attended, "tensor", split_axis=1, concat_axis=0, tiled=True)
    head_values = jnp.einsum(
        "thl,hlv->thv", by_head, value_proj, preferred_element_type=jnp.float32
    ).astype(jnp.bfloat16)
    head_values = head_values.reshape(
        head_values.shape[0], head_values.shape[1] * head_values.shape[2]
    )
    all_values = lax.all_gather(head_values, "dp", axis=0, tiled=True)
    down_pack, all_values = lax.optimization_barrier((down_pack, all_values))
    partial = jnp.dot(all_values, out_proj, preferred_element_type=jnp.float32)
    half = partial.shape[0] // 2
    role_idx = lax.axis_index("role")
    keep = lax.dynamic_slice_in_dim(partial, role_idx * half, half, 0)
    give = lax.dynamic_slice_in_dim(partial, (1 - role_idx) * half, half, 0)
    partial = keep + lax.ppermute(give, "role", [(0, 1), (1, 0)])
    n_tensor = lax.axis_size("tensor")
    partial = partial.reshape(n_tensor, partial.shape[0] // n_tensor, partial.shape[1])
    partial = lax.all_to_all(partial, "tensor", split_axis=0, concat_axis=0, tiled=True)
    attention = jnp.sum(partial, axis=0)
    mixed_in = lax.optimization_barrier(
        (residual.astype(jnp.float32) + attention).astype(jnp.bfloat16)
    )

    full_rows = lax.all_gather(mixed_in.reshape(-1, 128), "dp", axis=0, tiled=True)
    full_rows = full_rows.reshape(-1, group_rows, mixed_in.shape[1])
    full_rows = jnp.transpose(full_rows, (1, 0, 2)).reshape(group_rows, model_width)
    normed = rms_rows(full_rows, norm_gain)
    picked = jnp.dot(
        mine.astype(jnp.bfloat16), normed, preferred_element_type=jnp.float32
    ).astype(jnp.bfloat16)
    collected_rows = lax.all_gather(picked, RT, axis=0, tiled=True)
    gate_scores = jnp.dot(collected_rows, expert_gate_weight[0], preferred_element_type=jnp.float32)
    upper_bound = jnp.dot(collected_rows, expert_up_weight[0], preferred_element_type=jnp.float32)
    hidden = (jax.nn.silu(gate_scores) * upper_bound).astype(jnp.bfloat16)

    lanes = hidden.shape[1]
    owner_block = jnp.zeros((8, lanes), jnp.bfloat16)
    owner_block = owner_block.at[0, :capacity].set(mine_owner.astype(jnp.bfloat16))
    hidden_ext = jnp.concatenate([hidden, owner_block], axis=0)
    gathered = lax.all_gather(hidden_ext, RT, axis=0, tiled=True)
    gathered = gathered.reshape(n_slices, hidden.shape[0] + 8, lanes)
    owners = gathered[:, hidden.shape[0], :capacity].astype(jnp.int32).reshape(n_slices * capacity)
    hidden_all = jnp.transpose(gathered[:, : hidden.shape[0]], (1, 0, 2)).reshape(hidden.shape[0], -1)
    down_pack = down_pack.reshape(n_slices * hidden_slice, col_width + tenants * rank)
    down_w = down_pack[:, :col_width]
    left_w = down_pack[:, col_width:].reshape(n_slices * hidden_slice, tenants, rank)
    base_output = jnp.dot(hidden_all, down_w, preferred_element_type=jnp.float32)
    owner_mask = (owners[:, None] == jnp.arange(TEN, dtype=jnp.int32)[None, :]).astype(jnp.float32)
    mixing = jnp.einsum(
        "sf,ftr->str", hidden_all, left_w, preferred_element_type=jnp.float32
    ) * owner_mask[:, :, None]
    delta = jnp.einsum(
        "str,trd->sd", mixing, right_w.astype(jnp.float32), precision=lax.Precision.HIGHEST
    )
    expert_out = (base_output - delta).astype(jnp.bfloat16)
    expert_out = expert_out.reshape(n_slices, capacity, col_width)
    by_group = lax.all_to_all(expert_out, RT, split_axis=0, concat_axis=0, tiled=True)
    by_expert = lax.all_to_all(by_group, "dp", split_axis=0, concat_axis=0, tiled=True)

    chosen = (routes[:, :, None] == labels[None, None, :]).astype(jnp.float32)
    gate_of = jnp.sum(gate_values[:, :, None] * chosen, axis=1)
    weighting = table.astype(jnp.float32) * gate_of.T[:, None, :]
    expert_part = jnp.einsum(
        "ecg,ecd->gd", weighting, by_expert.astype(jnp.float32), precision=lax.Precision.HIGHEST
    )
    return (mixed_in.astype(jnp.float32) + expert_part).astype(jnp.bfloat16)


def solution(mesh):
    placed = (
        P(("dp", "tensor"), "role", None),
        P(("dp", "tensor"), None, None),
        P(("dp", "tensor"), None),
        P(("dp", "tensor")),
        P(("role", "tensor"), None, None),
        P(("role", "tensor"), "dp"),
        P(("role", "tensor"), "dp"),
        P(),
        P(("role", "tensor"), None),
        P(("role", "tensor"), None),
        P(("role", "tensor")),
        P("dp", None, ("role", "tensor")),
        P("dp", None, ("role", "tensor")),
        P("dp", ("role", "tensor"), None),
        P(None, "dp", ("role", "tensor"), None),
        P(None, "dp", None, None),
    )
    return jax.shard_map(
        local, mesh=mesh, in_specs=placed, out_specs=P(("role", "tensor"), "dp"), check_vma=False
    )
```

```python
import jax
import jax.numpy as jnp
from jax import lax
from jax.sharding import PartitionSpec as P

LAT = 512
EXPERTS = 16
TEN = 3


SCORE_SCALE = 0.07216878364870323
NORM_EPS = 1e-06
MASKED = -1e30
RT = ("role", "tensor")


def rms_rows(input_rows, norm_gain):
    wide = input_rows.astype(jnp.float32)
    scale = lax.rsqrt(jnp.mean(wide * wide, axis=-1, keepdims=True) + NORM_EPS)
    return (wide * scale * norm_gain.astype(jnp.float32)).astype(jnp.bfloat16)


def slot_table(routes, expert, capacity):
    hit = jnp.any(routes == expert, axis=-1).astype(jnp.int32)
    earlier = jnp.cumsum(hit, axis=-1) - hit
    slot_ids = jnp.arange(capacity, dtype=jnp.int32)
    return (hit[..., None, :] > 0) & (earlier[..., None, :] == slot_ids[:, None])


def local(
    queries,
    latent_cache,
    new_latent,
    cache_lengths,
    value_proj,
    out_proj,
    residual,
    norm_gain,
    routes,
    gate_values,
    tenant_ids,
    expert_gate_weight,
    expert_up_weight,
    expert_down_weight,
    left_delta_factor,
    factor_right,
):
    n_slices = lax.axis_size(RT)
    slice_idx = lax.axis_index(RT)
    group_rows = residual.shape[0]
    capacity = 5 * group_rows // 8
    model_width = expert_down_weight.shape[2]
    col_width = model_width // n_slices

    expert = lax.axis_index("dp")
    labels = jnp.arange(EXPERTS, dtype=jnp.int32)
    table = slot_table(routes, labels[:, None, None], capacity)
    mine = lax.dynamic_index_in_dim(table, expert, 0, keepdims=False)
    mine_owner = jnp.sum(mine.astype(jnp.int32) * tenant_ids[None, :], axis=1)
    hidden_slice = expert_down_weight.shape[1]
    down_local = expert_down_weight[0].reshape(hidden_slice, n_slices, col_width)
    left_local = left_delta_factor[:, 0]
    tenants, _, rank = left_local.shape
    left_local = jnp.transpose(left_local, (1, 0, 2)).reshape(hidden_slice, 1, tenants * rank)
    left_local = jnp.broadcast_to(left_local, (hidden_slice, n_slices, tenants * rank))
    down_pack = jnp.concatenate([down_local, left_local], axis=2)
    pack_width = down_pack.shape[2]
    info = mine_owner.astype(jnp.bfloat16)
    info_rows = jnp.zeros((8, pack_width), jnp.bfloat16).at[0, : info.shape[0]].set(info)
    info_rows = jnp.broadcast_to(info_rows[:, None, :], (8, n_slices, pack_width))
    down_pack = jnp.concatenate([down_pack, info_rows], axis=0)
    down_pack = lax.all_to_all(down_pack, RT, split_axis=1, concat_axis=0, tiled=True)
    right_w = lax.dynamic_slice_in_dim(factor_right[:, 0], slice_idx * col_width, col_width, 2)

    seq_count, context, width = latent_cache.shape
    local_heads = queries.shape[1]
    paired = queries.reshape(seq_count, 2, local_heads, width)
    scores = (
        jnp.einsum("sqhd,spd->sqhp", paired, latent_cache, preferred_element_type=jnp.float32)
        * SCORE_SCALE
    )
    present = jnp.arange(context, dtype=jnp.int32)[None, :] < cache_lengths[:, None]
    scores = jnp.where(present[:, None, None, :], scores, MASKED)
    fresh_keys = new_latent.reshape(seq_count, 2, width)
    fresh = (
        jnp.einsum("sqhd,skd->sqhk", paired, fresh_keys, preferred_element_type=jnp.float32)
        * SCORE_SCALE
    )
    causal = jnp.arange(2)[:, None] >= jnp.arange(2)[None, :]
    fresh = jnp.where(causal[None, :, None, :], fresh, MASKED)
    top = jnp.maximum(jnp.max(scores, axis=3), jnp.max(fresh, axis=3))[..., None]
    weights = jnp.exp(scores - top)
    fresh_weights = jnp.exp(fresh - top)
    total = jnp.sum(weights, axis=3) + jnp.sum(fresh_weights, axis=3)
    summed = jnp.einsum(
        "sqhp,spd->sqhd",
        weights.astype(jnp.bfloat16),
        latent_cache[:, :, :LAT],
        preferred_element_type=jnp.float32,
    )
    summed = summed + jnp.einsum(
        "sqhk,skd->sqhd",
        fresh_weights.astype(jnp.bfloat16),
        fresh_keys[:, :, :LAT],
        preferred_element_type=jnp.float32,
    )
    attended = (
        (summed / total[..., None]).astype(jnp.bfloat16).reshape(seq_count * 2, local_heads, LAT)
    )
    by_head = lax.all_to_all(attended, "tensor", split_axis=1, concat_axis=0, tiled=True)
    head_values = jnp.einsum(
        "thl,hlv->thv", by_head, value_proj, preferred_element_type=jnp.float32
    ).astype(jnp.bfloat16)
    head_values = head_values.reshape(
        head_values.shape[0], head_values.shape[1] * head_values.shape[2]
    )
    all_values = lax.all_gather(head_values, "dp", axis=0, tiled=True)
    down_pack = down_pack.reshape(n_slices, hidden_slice + 8, pack_width)
    owners = down_pack[:, hidden_slice, :capacity].astype(jnp.int32).reshape(n_slices * capacity)
    down_pack = down_pack[:, :hidden_slice].reshape(n_slices * hidden_slice, pack_width)
    down_w = down_pack[:, :col_width]
    left_w = down_pack[:, col_width:].reshape(n_slices * hidden_slice, tenants, rank)
    down_w, left_w, owners, all_values = lax.optimization_barrier((down_w, left_w, owners, all_values))
    partial = jnp.dot(all_values, out_proj, preferred_element_type=jnp.float32)
    half = partial.shape[0] // 2
    role_idx = lax.axis_index("role")
    keep = lax.dynamic_slice_in_dim(partial, role_idx * half, half, 0)
    give = lax.dynamic_slice_in_dim(partial, (1 - role_idx) * half, half, 0)
    partial = keep + lax.ppermute(give, "role", [(0, 1), (1, 0)])
    n_tensor = lax.axis_size("tensor")
    partial = partial.reshape(n_tensor, partial.shape[0] // n_tensor, partial.shape[1])
    partial = lax.all_to_all(partial, "tensor", split_axis=0, concat_axis=0, tiled=True)
    attention = jnp.sum(partial, axis=0)
    mixed_in = lax.optimization_barrier(
        (residual.astype(jnp.float32) + attention).astype(jnp.bfloat16)
    )

    full_rows = lax.all_gather(mixed_in, "dp", axis=0, tiled=True)
    full_rows = full_rows.reshape(-1, group_rows, mixed_in.shape[1])
    full_rows = jnp.transpose(full_rows, (1, 0, 2)).reshape(group_rows, model_width)
    normed = rms_rows(full_rows, norm_gain)
    picked = jnp.dot(
        mine.astype(jnp.bfloat16), normed, preferred_element_type=jnp.float32
    ).astype(jnp.bfloat16)
    collected_rows = lax.all_gather(picked, RT, axis=0, tiled=True)
    gate_scores = jnp.dot(collected_rows, expert_gate_weight[0], preferred_element_type=jnp.float32)
    upper_bound = jnp.dot(collected_rows, expert_up_weight[0], preferred_element_type=jnp.float32)
    hidden = (jax.nn.silu(gate_scores) * upper_bound).astype(jnp.bfloat16)

    gathered = lax.all_gather(hidden, RT, axis=0, tiled=False)
    hidden_all = jnp.transpose(gathered, (1, 0, 2)).reshape(hidden.shape[0], -1)
    base_output = jnp.dot(hidden_all, down_w, preferred_element_type=jnp.float32)
    owner_mask = (owners[:, None] == jnp.arange(TEN, dtype=jnp.int32)[None, :]).astype(jnp.float32)
    mixing = jnp.einsum(
        "sf,ftr->str", hidden_all, left_w, preferred_element_type=jnp.float32
    ) * owner_mask[:, :, None]
    delta = jnp.einsum(
        "str,trd->sd", mixing, right_w.astype(jnp.float32), precision=lax.Precision.HIGHEST
    )
    expert_out = (base_output - delta).astype(jnp.bfloat16)
    expert_out = expert_out.reshape(n_slices, capacity, col_width)
    by_group = lax.all_to_all(expert_out, RT, split_axis=0, concat_axis=0, tiled=True)
    by_expert = lax.all_to_all(by_group, "dp", split_axis=0, concat_axis=0, tiled=True)

    chosen = (routes[:, :, None] == labels[None, None, :]).astype(jnp.float32)
    gate_of = jnp.sum(gate_values[:, :, None] * chosen, axis=1)
    weighting = table.astype(jnp.float32) * gate_of.T[:, None, :]
    expert_part = jnp.einsum(
        "ecg,ecd->gd", weighting, by_expert.astype(jnp.float32), precision=lax.Precision.HIGHEST
    )
    return (mixed_in.astype(jnp.float32) + expert_part).astype(jnp.bfloat16)


def solution(mesh):
    placed = (
        P(("dp", "tensor"), "role", None),
        P(("dp", "tensor"), None, None),
        P(("dp", "tensor"), None),
        P(("dp", "tensor")),
        P(("role", "tensor"), None, None),
        P(("role", "tensor"), "dp"),
        P(("role", "tensor"), "dp"),
        P(),
        P(("role", "tensor"), None),
        P(("role", "tensor"), None),
        P(("role", "tensor")),
        P("dp", None, ("role", "tensor")),
        P("dp", None, ("role", "tensor")),
        P("dp", ("role", "tensor"), None),
        P(None, "dp", ("role", "tensor"), None),
        P(None, "dp", None, None),
    )
    return jax.shard_map(
        local, mesh=mesh, in_specs=placed, out_specs=P(("role", "tensor"), "dp"), check_vma=False
    )
```

```python
import jax
import jax.numpy as jnp
from jax import lax
from jax.sharding import PartitionSpec as P

LAT = 512
EXPERTS = 16
TEN = 3


SCORE_SCALE = 0.07216878364870323
NORM_EPS = 1e-06
MASKED = -1e30
RT = ("role", "tensor")


def rms_rows(input_rows, norm_gain):
    wide = input_rows.astype(jnp.float32)
    scale = lax.rsqrt(jnp.mean(wide * wide, axis=-1, keepdims=True) + NORM_EPS)
    return (wide * scale * norm_gain.astype(jnp.float32)).astype(jnp.bfloat16)


def slot_table(routes, expert, capacity):
    hit = jnp.any(routes == expert, axis=-1).astype(jnp.int32)
    earlier = jnp.cumsum(hit, axis=-1) - hit
    slot_ids = jnp.arange(capacity, dtype=jnp.int32)
    return (hit[..., None, :] > 0) & (earlier[..., None, :] == slot_ids[:, None])


def local(
    queries,
    latent_cache,
    new_latent,
    cache_lengths,
    value_proj,
    out_proj,
    residual,
    norm_gain,
    routes,
    gate_values,
    tenant_ids,
    expert_gate_weight,
    expert_up_weight,
    expert_down_weight,
    left_delta_factor,
    factor_right,
):
    n_slices = lax.axis_size(RT)
    slice_idx = lax.axis_index(RT)
    group_rows = residual.shape[0]
    capacity = 5 * group_rows // 8
    model_width = expert_down_weight.shape[2]
    col_width = model_width // n_slices

    expert = lax.axis_index("dp")
    labels = jnp.arange(EXPERTS, dtype=jnp.int32)
    table = slot_table(routes, labels[:, None, None], capacity)
    mine = lax.dynamic_index_in_dim(table, expert, 0, keepdims=False)
    mine_owner = jnp.sum(mine.astype(jnp.int32) * tenant_ids[None, :], axis=1)
    hidden_slice = expert_down_weight.shape[1]
    down_local = expert_down_weight[0].reshape(hidden_slice, n_slices, col_width)
    down_local = jnp.transpose(down_local, (1, 0, 2))
    left_local = left_delta_factor[:, 0]
    tenants, _, rank = left_local.shape
    left_local = jnp.transpose(left_local, (1, 0, 2)).reshape(1, hidden_slice, tenants * rank)
    left_local = jnp.broadcast_to(left_local, (n_slices, hidden_slice, tenants * rank))
    down_pack = jnp.concatenate([down_local, left_local], axis=2)
    pack_width = down_pack.shape[2]
    info = mine_owner.astype(jnp.bfloat16)
    info_rows = jnp.zeros((8, pack_width), jnp.bfloat16).at[0, : info.shape[0]].set(info)
    info_rows = jnp.broadcast_to(info_rows[None], (n_slices, 8, pack_width))
    down_pack = jnp.concatenate([down_pack, info_rows], axis=1)
    down_pack = lax.all_to_all(down_pack, RT, split_axis=0, concat_axis=0, tiled=True)
    right_w = lax.dynamic_slice_in_dim(factor_right[:, 0], slice_idx * col_width, col_width, 2)

    seq_count, context, width = latent_cache.shape
    local_heads = queries.shape[1]
    paired = queries.reshape(seq_count, 2, local_heads, width)
    scores = (
        jnp.einsum("sqhd,spd->sqhp", paired, latent_cache, preferred_element_type=jnp.float32)
        * SCORE_SCALE
    )
    present = jnp.arange(context, dtype=jnp.int32)[None, :] < cache_lengths[:, None]
    scores = jnp.where(present[:, None, None, :], scores, MASKED)
    fresh_keys = new_latent.reshape(seq_count, 2, width)
    fresh = (
        jnp.einsum("sqhd,skd->sqhk", paired, fresh_keys, preferred_element_type=jnp.float32)
        * SCORE_SCALE
    )
    causal = jnp.arange(2)[:, None] >= jnp.arange(2)[None, :]
    fresh = jnp.where(causal[None, :, None, :], fresh, MASKED)
    top = jnp.maximum(jnp.max(scores, axis=3), jnp.max(fresh, axis=3))[..., None]
    weights = jnp.exp(scores - top)
    fresh_weights = jnp.exp(fresh - top)
    total = jnp.sum(weights, axis=3) + jnp.sum(fresh_weights, axis=3)
    summed = jnp.einsum(
        "sqhp,spd->sqhd",
        weights.astype(jnp.bfloat16),
        latent_cache[:, :, :LAT],
        preferred_element_type=jnp.float32,
    )
    summed = summed + jnp.einsum(
        "sqhk,skd->sqhd",
        fresh_weights.astype(jnp.bfloat16),
        fresh_keys[:, :, :LAT],
        preferred_element_type=jnp.float32,
    )
    attended = (
        (summed / total[..., None]).astype(jnp.bfloat16).reshape(seq_count * 2, local_heads, LAT)
    )
    by_head = lax.all_to_all(attended, "tensor", split_axis=1, concat_axis=0, tiled=True)
    head_values = jnp.einsum(
        "thl,hlv->thv", by_head, value_proj, preferred_element_type=jnp.float32
    ).astype(jnp.bfloat16)
    head_values = head_values.reshape(
        head_values.shape[0], head_values.shape[1] * head_values.shape[2]
    )
    all_values = lax.all_gather(head_values, "dp", axis=0, tiled=True)
    owners = down_pack[:, hidden_slice, :capacity].astype(jnp.int32).reshape(n_slices * capacity)
    down_pack = down_pack[:, :hidden_slice].reshape(n_slices * hidden_slice, pack_width)
    down_w = down_pack[:, :col_width]
    left_w = down_pack[:, col_width:].reshape(n_slices * hidden_slice, tenants, rank)
    down_w, left_w, owners, all_values = lax.optimization_barrier((down_w, left_w, owners, all_values))
    partial = jnp.dot(all_values, out_proj, preferred_element_type=jnp.float32)
    half = partial.shape[0] // 2
    role_idx = lax.axis_index("role")
    keep = lax.dynamic_slice_in_dim(partial, role_idx * half, half, 0)
    give = lax.dynamic_slice_in_dim(partial, (1 - role_idx) * half, half, 0)
    partial = keep + lax.ppermute(give, "role", [(0, 1), (1, 0)])
    n_tensor = lax.axis_size("tensor")
    partial = partial.reshape(n_tensor, partial.shape[0] // n_tensor, partial.shape[1])
    partial = lax.all_to_all(partial.astype(jnp.bfloat16), "tensor", split_axis=0, concat_axis=0, tiled=True)
    attention = jnp.sum(partial.astype(jnp.float32), axis=0)
    mixed_in = lax.optimization_barrier(
        (residual.astype(jnp.float32) + attention).astype(jnp.bfloat16)
    )

    full_rows = lax.all_gather(mixed_in, "dp", axis=0, tiled=True)
    full_rows = full_rows.reshape(-1, group_rows, mixed_in.shape[1])
    full_rows = jnp.transpose(full_rows, (1, 0, 2)).reshape(group_rows, model_width)
    normed = rms_rows(full_rows, norm_gain)
    picked = jnp.dot(
        mine.astype(jnp.bfloat16), normed, preferred_element_type=jnp.float32
    ).astype(jnp.bfloat16)
    collected_rows = lax.all_gather(picked, RT, axis=0, tiled=True)
    gate_scores = jnp.dot(collected_rows, expert_gate_weight[0], preferred_element_type=jnp.float32)
    upper_bound = jnp.dot(collected_rows, expert_up_weight[0], preferred_element_type=jnp.float32)
    hidden = (jax.nn.silu(gate_scores) * upper_bound).astype(jnp.bfloat16)

    gathered = lax.all_gather(hidden, RT, axis=0, tiled=False)
    hidden_all = jnp.transpose(gathered, (1, 0, 2)).reshape(hidden.shape[0], -1)
    base_output = jnp.dot(hidden_all, down_w, preferred_element_type=jnp.float32)
    owner_mask = (owners[:, None] == jnp.arange(TEN, dtype=jnp.int32)[None, :]).astype(jnp.float32)
    mixing = jnp.einsum(
        "sf,ftr->str", hidden_all, left_w, preferred_element_type=jnp.float32
    ) * owner_mask[:, :, None]
    delta = jnp.einsum(
        "str,trd->sd", mixing, right_w.astype(jnp.float32), precision=lax.Precision.HIGHEST
    )
    expert_out = (base_output - delta).astype(jnp.bfloat16)
    expert_out = expert_out.reshape(n_slices, capacity, col_width)
    by_group = lax.all_to_all(expert_out, RT, split_axis=0, concat_axis=0, tiled=True)
    by_expert = lax.all_to_all(by_group, "dp", split_axis=0, concat_axis=0, tiled=True)

    chosen = (routes[:, :, None] == labels[None, None, :]).astype(jnp.float32)
    gate_of = jnp.sum(gate_values[:, :, None] * chosen, axis=1)
    weighting = table.astype(jnp.float32) * gate_of.T[:, None, :]
    expert_part = jnp.einsum(
        "ecg,ecd->gd", weighting, by_expert.astype(jnp.float32), precision=lax.Precision.HIGHEST
    )
    return (mixed_in.astype(jnp.float32) + expert_part).astype(jnp.bfloat16)


def solution(mesh):
    placed = (
        P(("dp", "tensor"), "role", None),
        P(("dp", "tensor"), None, None),
        P(("dp", "tensor"), None),
        P(("dp", "tensor")),
        P(("role", "tensor"), None, None),
        P(("role", "tensor"), "dp"),
        P(("role", "tensor"), "dp"),
        P(),
        P(("role", "tensor"), None),
        P(("role", "tensor"), None),
        P(("role", "tensor")),
        P("dp", None, ("role", "tensor")),
        P("dp", None, ("role", "tensor")),
        P("dp", ("role", "tensor"), None),
        P(None, "dp", ("role", "tensor"), None),
        P(None, "dp", None, None),
    )
    return jax.shard_map(
        local, mesh=mesh, in_specs=placed, out_specs=P(("role", "tensor"), "dp"), check_vma=False
    )
```

```python
import jax
import jax.numpy as jnp
from jax import lax
from jax.sharding import PartitionSpec as P

LAT = 512
EXPERTS = 16
TEN = 3


SCORE_SCALE = 0.07216878364870323
NORM_EPS = 1e-06
MASKED = -1e30
RT = ("role", "tensor")


def rms_rows(input_rows, norm_gain):
    wide = input_rows.astype(jnp.float32)
    scale = lax.rsqrt(jnp.mean(wide * wide, axis=-1, keepdims=True) + NORM_EPS)
    return (wide * scale * norm_gain.astype(jnp.float32)).astype(jnp.bfloat16)


def slot_table(routes, expert, capacity):
    hit = jnp.any(routes == expert, axis=-1).astype(jnp.int32)
    earlier = jnp.cumsum(hit, axis=-1) - hit
    slot_ids = jnp.arange(capacity, dtype=jnp.int32)
    return (hit[..., None, :] > 0) & (earlier[..., None, :] == slot_ids[:, None])


def local(
    queries,
    latent_cache,
    new_latent,
    cache_lengths,
    value_proj,
    out_proj,
    residual,
    norm_gain,
    routes,
    gate_values,
    tenant_ids,
    expert_gate_weight,
    expert_up_weight,
    expert_down_weight,
    left_delta_factor,
    factor_right,
):
    n_slices = lax.axis_size(RT)
    slice_idx = lax.axis_index(RT)
    group_rows = residual.shape[0]
    capacity = 5 * group_rows // 8
    model_width = expert_down_weight.shape[2]
    col_width = model_width // n_slices

    expert = lax.axis_index("dp")
    labels = jnp.arange(EXPERTS, dtype=jnp.int32)
    table = slot_table(routes, labels[:, None, None], capacity)
    mine = lax.dynamic_index_in_dim(table, expert, 0, keepdims=False)
    mine_owner = jnp.sum(mine.astype(jnp.int32) * tenant_ids[None, :], axis=1)
    hidden_slice = expert_down_weight.shape[1]
    down_local = expert_down_weight[0].reshape(hidden_slice, n_slices, col_width)
    down_local = jnp.transpose(down_local, (1, 0, 2))
    left_local = left_delta_factor[:, 0]
    tenants, _, rank = left_local.shape
    left_local = jnp.transpose(left_local, (1, 0, 2)).reshape(1, hidden_slice, tenants * rank)
    left_local = jnp.broadcast_to(left_local, (n_slices, hidden_slice, tenants * rank))
    down_pack = jnp.concatenate([down_local, left_local], axis=2)
    pack_width = down_pack.shape[2]
    info = mine_owner.astype(jnp.bfloat16)
    info_rows = jnp.zeros((8, pack_width), jnp.bfloat16).at[0, : info.shape[0]].set(info)
    info_rows = jnp.broadcast_to(info_rows[None], (n_slices, 8, pack_width))
    down_pack = jnp.concatenate([down_pack, info_rows], axis=1)
    down_pack = lax.all_to_all(down_pack, RT, split_axis=0, concat_axis=0, tiled=True)
    right_w = lax.dynamic_slice_in_dim(factor_right[:, 0], slice_idx * col_width, col_width, 2)

    seq_count, context, width = latent_cache.shape
    local_heads = queries.shape[1]
    paired = queries.reshape(seq_count, 2, local_heads, width)
    scores = (
        jnp.einsum("sqhd,spd->sqhp", paired, latent_cache, preferred_element_type=jnp.float32)
        * SCORE_SCALE
    )
    present = jnp.arange(context, dtype=jnp.int32)[None, :] < cache_lengths[:, None]
    scores = jnp.where(present[:, None, None, :], scores, MASKED)
    fresh_keys = new_latent.reshape(seq_count, 2, width)
    fresh = (
        jnp.einsum("sqhd,skd->sqhk", paired, fresh_keys, preferred_element_type=jnp.float32)
        * SCORE_SCALE
    )
    causal = jnp.arange(2)[:, None] >= jnp.arange(2)[None, :]
    fresh = jnp.where(causal[None, :, None, :], fresh, MASKED)
    top = jnp.maximum(jnp.max(scores, axis=3), jnp.max(fresh, axis=3))[..., None]
    weights = jnp.exp(scores - top)
    fresh_weights = jnp.exp(fresh - top)
    total = jnp.sum(weights, axis=3) + jnp.sum(fresh_weights, axis=3)
    summed = jnp.einsum(
        "sqhp,spd->sqhd",
        weights.astype(jnp.bfloat16),
        latent_cache[:, :, :LAT],
        preferred_element_type=jnp.float32,
    )
    summed = summed + jnp.einsum(
        "sqhk,skd->sqhd",
        fresh_weights.astype(jnp.bfloat16),
        fresh_keys[:, :, :LAT],
        preferred_element_type=jnp.float32,
    )
    attended = (
        (summed / total[..., None]).astype(jnp.bfloat16).reshape(seq_count * 2, local_heads, LAT)
    )
    by_head = lax.all_to_all(attended, "tensor", split_axis=1, concat_axis=0, tiled=True)
    head_values = jnp.einsum(
        "thl,hlv->thv", by_head, value_proj, preferred_element_type=jnp.float32
    ).astype(jnp.bfloat16)
    head_values = head_values.reshape(
        head_values.shape[0], head_values.shape[1] * head_values.shape[2]
    )
    all_values = lax.all_gather(head_values, "dp", axis=0, tiled=True)
    owners = down_pack[:, hidden_slice, :capacity].astype(jnp.int32).reshape(n_slices * capacity)
    down_pack = down_pack[:, :hidden_slice].reshape(n_slices * hidden_slice, pack_width)
    down_w = down_pack[:, :col_width]
    left_w = down_pack[:, col_width:].reshape(n_slices * hidden_slice, tenants, rank)
    down_w, left_w, owners, all_values = lax.optimization_barrier((down_w, left_w, owners, all_values))
    partial = jnp.dot(all_values, out_proj, preferred_element_type=jnp.float32)
    half = partial.shape[0] // 2
    role_idx = lax.axis_index("role")
    keep = lax.dynamic_slice_in_dim(partial, role_idx * half, half, 0)
    give = lax.dynamic_slice_in_dim(partial, (1 - role_idx) * half, half, 0)
    partial = keep + lax.ppermute(give, "role", [(0, 1), (1, 0)])
    n_tensor = lax.axis_size("tensor")
    partial = partial.reshape(n_tensor, partial.shape[0] // n_tensor, partial.shape[1])
    partial = lax.all_to_all(partial.astype(jnp.bfloat16), "tensor", split_axis=0, concat_axis=0, tiled=True)
    attention = jnp.sum(partial.astype(jnp.float32), axis=0)
    mixed_in = lax.optimization_barrier(
        (residual.astype(jnp.float32) + attention).astype(jnp.bfloat16)
    )

    n_dp = lax.axis_size("dp")
    spread = jnp.broadcast_to(mixed_in[None], (n_dp,) + mixed_in.shape)
    full_rows = lax.all_to_all(spread, "dp", split_axis=0, concat_axis=0, tiled=True)
    full_rows = full_rows.reshape(-1, group_rows, mixed_in.shape[1])
    full_rows = jnp.transpose(full_rows, (1, 0, 2)).reshape(group_rows, model_width)
    normed = rms_rows(full_rows, norm_gain)
    picked = jnp.dot(
        mine.astype(jnp.bfloat16), normed, preferred_element_type=jnp.float32
    ).astype(jnp.bfloat16)
    collected_rows = lax.all_gather(picked, RT, axis=0, tiled=True)
    gate_scores = jnp.dot(collected_rows, expert_gate_weight[0], preferred_element_type=jnp.float32)
    upper_bound = jnp.dot(collected_rows, expert_up_weight[0], preferred_element_type=jnp.float32)
    hidden = (jax.nn.silu(gate_scores) * upper_bound).astype(jnp.bfloat16)

    gathered = lax.all_gather(hidden, RT, axis=0, tiled=False)
    hidden_all = jnp.transpose(gathered, (1, 0, 2)).reshape(hidden.shape[0], -1)
    base_output = jnp.dot(hidden_all, down_w, preferred_element_type=jnp.float32)
    owner_mask = (owners[:, None] == jnp.arange(TEN, dtype=jnp.int32)[None, :]).astype(jnp.float32)
    mixing = jnp.einsum(
        "sf,ftr->str", hidden_all, left_w, preferred_element_type=jnp.float32
    ) * owner_mask[:, :, None]
    delta = jnp.einsum(
        "str,trd->sd", mixing, right_w.astype(jnp.float32), precision=lax.Precision.HIGHEST
    )
    expert_out = (base_output - delta).astype(jnp.bfloat16)
    expert_out = expert_out.reshape(n_slices, capacity, col_width)
    by_group = lax.all_to_all(expert_out, RT, split_axis=0, concat_axis=0, tiled=True)
    by_expert = lax.all_to_all(by_group, "dp", split_axis=0, concat_axis=0, tiled=True)

    chosen = (routes[:, :, None] == labels[None, None, :]).astype(jnp.float32)
    gate_of = jnp.sum(gate_values[:, :, None] * chosen, axis=1)
    weighting = table.astype(jnp.float32) * gate_of.T[:, None, :]
    expert_part = jnp.einsum(
        "ecg,ecd->gd", weighting, by_expert.astype(jnp.float32), precision=lax.Precision.HIGHEST
    )
    return (mixed_in.astype(jnp.float32) + expert_part).astype(jnp.bfloat16)


def solution(mesh):
    placed = (
        P(("dp", "tensor"), "role", None),
        P(("dp", "tensor"), None, None),
        P(("dp", "tensor"), None),
        P(("dp", "tensor")),
        P(("role", "tensor"), None, None),
        P(("role", "tensor"), "dp"),
        P(("role", "tensor"), "dp"),
        P(),
        P(("role", "tensor"), None),
        P(("role", "tensor"), None),
        P(("role", "tensor")),
        P("dp", None, ("role", "tensor")),
        P("dp", None, ("role", "tensor")),
        P("dp", ("role", "tensor"), None),
        P(None, "dp", ("role", "tensor"), None),
        P(None, "dp", None, None),
    )
    return jax.shard_map(
        local, mesh=mesh, in_specs=placed, out_specs=P(("role", "tensor"), "dp"), check_vma=False
    )
```

```python
import jax
import jax.numpy as jnp
from jax import lax
from jax.sharding import PartitionSpec as P

LAT = 512
EXPERTS = 16
TEN = 3


SCORE_SCALE = 0.07216878364870323
NORM_EPS = 1e-06
MASKED = -1e30
RT = ("role", "tensor")


def rms_rows(input_rows, norm_gain):
    wide = input_rows.astype(jnp.float32)
    scale = lax.rsqrt(jnp.mean(wide * wide, axis=-1, keepdims=True) + NORM_EPS)
    return (wide * scale * norm_gain.astype(jnp.float32)).astype(jnp.bfloat16)


def slot_table(routes, expert, capacity):
    hit = jnp.any(routes == expert, axis=-1).astype(jnp.int32)
    earlier = jnp.cumsum(hit, axis=-1) - hit
    slot_ids = jnp.arange(capacity, dtype=jnp.int32)
    return (hit[..., None, :] > 0) & (earlier[..., None, :] == slot_ids[:, None])


def local(
    queries,
    latent_cache,
    new_latent,
    cache_lengths,
    value_proj,
    out_proj,
    residual,
    norm_gain,
    routes,
    gate_values,
    tenant_ids,
    expert_gate_weight,
    expert_up_weight,
    expert_down_weight,
    left_delta_factor,
    factor_right,
):
    n_slices = lax.axis_size(RT)
    slice_idx = lax.axis_index(RT)
    group_rows = residual.shape[0]
    capacity = 5 * group_rows // 8
    model_width = expert_down_weight.shape[2]
    col_width = model_width // n_slices

    expert = lax.axis_index("dp")
    labels = jnp.arange(EXPERTS, dtype=jnp.int32)
    table = slot_table(routes, labels[:, None, None], capacity)
    mine = lax.dynamic_index_in_dim(table, expert, 0, keepdims=False)
    mine_owner = jnp.sum(mine.astype(jnp.int32) * tenant_ids[None, :], axis=1)
    hidden_slice = expert_down_weight.shape[1]
    down_local = expert_down_weight[0].reshape(hidden_slice, n_slices, col_width)
    down_local = jnp.transpose(down_local, (1, 0, 2))
    left_local = left_delta_factor[:, 0]
    tenants, _, rank = left_local.shape
    left_local = jnp.transpose(left_local, (1, 0, 2)).reshape(1, hidden_slice, tenants * rank)
    left_local = jnp.broadcast_to(left_local, (n_slices, hidden_slice, tenants * rank))
    down_pack = jnp.concatenate([down_local, left_local], axis=2)
    pack_width = down_pack.shape[2]
    info = mine_owner.astype(jnp.bfloat16)
    info_rows = jnp.zeros((8, pack_width), jnp.bfloat16).at[0, : info.shape[0]].set(info)
    info_rows = jnp.broadcast_to(info_rows[None], (n_slices, 8, pack_width))
    down_pack = jnp.concatenate([down_pack, info_rows], axis=1)
    down_pack = lax.all_to_all(down_pack, RT, split_axis=0, concat_axis=0, tiled=True)
    right_w = lax.dynamic_slice_in_dim(factor_right[:, 0], slice_idx * col_width, col_width, 2)

    seq_count, context, width = latent_cache.shape
    local_heads = queries.shape[1]
    paired = queries.reshape(seq_count, 2, local_heads, width)
    scores = (
        jnp.einsum("sqhd,spd->sqhp", paired, latent_cache, preferred_element_type=jnp.float32)
        * SCORE_SCALE
    )
    present = jnp.arange(context, dtype=jnp.int32)[None, :] < cache_lengths[:, None]
    scores = jnp.where(present[:, None, None, :], scores, MASKED)
    fresh_keys = new_latent.reshape(seq_count, 2, width)
    fresh = (
        jnp.einsum("sqhd,skd->sqhk", paired, fresh_keys, preferred_element_type=jnp.float32)
        * SCORE_SCALE
    )
    causal = jnp.arange(2)[:, None] >= jnp.arange(2)[None, :]
    fresh = jnp.where(causal[None, :, None, :], fresh, MASKED)
    top = jnp.maximum(jnp.max(scores, axis=3), jnp.max(fresh, axis=3))[..., None]
    weights = jnp.exp(scores - top)
    fresh_weights = jnp.exp(fresh - top)
    total = jnp.sum(weights, axis=3) + jnp.sum(fresh_weights, axis=3)
    summed = jnp.einsum(
        "sqhp,spd->sqhd",
        weights.astype(jnp.bfloat16),
        latent_cache[:, :, :LAT],
        preferred_element_type=jnp.float32,
    )
    summed = summed + jnp.einsum(
        "sqhk,skd->sqhd",
        fresh_weights.astype(jnp.bfloat16),
        fresh_keys[:, :, :LAT],
        preferred_element_type=jnp.float32,
    )
    attended = (
        (summed / total[..., None]).astype(jnp.bfloat16).reshape(seq_count * 2, local_heads, LAT)
    )
    by_head = lax.all_to_all(attended, "tensor", split_axis=1, concat_axis=0, tiled=True)
    head_values = jnp.einsum(
        "thl,hlv->thv", by_head, value_proj, preferred_element_type=jnp.float32
    ).astype(jnp.bfloat16)
    head_values = head_values.reshape(
        head_values.shape[0], head_values.shape[1] * head_values.shape[2]
    )
    all_values = lax.all_gather(head_values, "dp", axis=0, tiled=True)
    owners = down_pack[:, hidden_slice, :capacity].astype(jnp.int32).reshape(n_slices * capacity)
    down_pack = down_pack[:, :hidden_slice].reshape(n_slices * hidden_slice, pack_width)
    down_w = down_pack[:, :col_width]
    left_w = down_pack[:, col_width:].reshape(n_slices * hidden_slice, tenants, rank)
    down_w, left_w, owners, all_values = lax.optimization_barrier((down_w, left_w, owners, all_values))
    partial = jnp.dot(all_values, out_proj, preferred_element_type=jnp.float32)
    half = partial.shape[0] // 2
    role_idx = lax.axis_index("role")
    keep = lax.dynamic_slice_in_dim(partial, role_idx * half, half, 0)
    give = lax.dynamic_slice_in_dim(partial, (1 - role_idx) * half, half, 0)
    partial = keep + lax.ppermute(give, "role", [(0, 1), (1, 0)])
    n_tensor = lax.axis_size("tensor")
    partial = partial.reshape(n_tensor, partial.shape[0] // n_tensor, partial.shape[1])
    partial = lax.all_to_all(partial.astype(jnp.bfloat16), "tensor", split_axis=0, concat_axis=0, tiled=True)
    attention = jnp.sum(partial.astype(jnp.float32), axis=0)
    mixed_in = lax.optimization_barrier(
        (residual.astype(jnp.float32) + attention).astype(jnp.bfloat16)
    )

    n_dp = lax.axis_size("dp")
    spread = jnp.broadcast_to(mixed_in[None], (n_dp,) + mixed_in.shape)
    full_rows = lax.all_to_all(spread, "dp", split_axis=0, concat_axis=0, tiled=True)
    full_rows = full_rows.reshape(-1, group_rows, mixed_in.shape[1])
    full_rows = jnp.transpose(full_rows, (1, 0, 2)).reshape(group_rows, model_width)
    normed = rms_rows(full_rows, norm_gain)
    picked = jnp.dot(
        mine.astype(jnp.bfloat16), normed, preferred_element_type=jnp.float32
    ).astype(jnp.bfloat16)
    collected_rows = lax.all_gather(picked, RT, axis=0, tiled=True)
    gate_scores = jnp.dot(collected_rows, expert_gate_weight[0], preferred_element_type=jnp.float32)
    upper_bound = jnp.dot(collected_rows, expert_up_weight[0], preferred_element_type=jnp.float32)
    hidden = (jax.nn.silu(gate_scores) * upper_bound).astype(jnp.bfloat16)

    gathered = lax.all_gather(hidden, RT, axis=0, tiled=False)
    down_w = down_w.reshape(n_slices, hidden_slice, col_width)
    left_w = left_w.reshape(n_slices, hidden_slice, tenants, rank)
    base_output = jnp.einsum("jsh,jhc->sc", gathered, down_w, preferred_element_type=jnp.float32)
    owner_mask = (owners[:, None] == jnp.arange(TEN, dtype=jnp.int32)[None, :]).astype(jnp.float32)
    mixing = jnp.einsum(
        "jsf,jftr->str", gathered, left_w, preferred_element_type=jnp.float32
    ) * owner_mask[:, :, None]
    delta = jnp.einsum(
        "str,trd->sd", mixing, right_w.astype(jnp.float32), precision=lax.Precision.HIGHEST
    )
    expert_out = (base_output - delta).astype(jnp.bfloat16)
    expert_out = expert_out.reshape(n_slices, capacity, col_width)
    by_group = lax.all_to_all(expert_out, RT, split_axis=0, concat_axis=0, tiled=True)
    by_expert = lax.all_to_all(by_group, "dp", split_axis=0, concat_axis=0, tiled=True)

    chosen = (routes[:, :, None] == labels[None, None, :]).astype(jnp.float32)
    gate_of = jnp.sum(gate_values[:, :, None] * chosen, axis=1)
    weighting = table.astype(jnp.float32) * gate_of.T[:, None, :]
    expert_part = jnp.einsum(
        "ecg,ecd->gd", weighting, by_expert.astype(jnp.float32), precision=lax.Precision.HIGHEST
    )
    return (mixed_in.astype(jnp.float32) + expert_part).astype(jnp.bfloat16)


def solution(mesh):
    placed = (
        P(("dp", "tensor"), "role", None),
        P(("dp", "tensor"), None, None),
        P(("dp", "tensor"), None),
        P(("dp", "tensor")),
        P(("role", "tensor"), None, None),
        P(("role", "tensor"), "dp"),
        P(("role", "tensor"), "dp"),
        P(),
        P(("role", "tensor"), None),
        P(("role", "tensor"), None),
        P(("role", "tensor")),
        P("dp", None, ("role", "tensor")),
        P("dp", None, ("role", "tensor")),
        P("dp", ("role", "tensor"), None),
        P(None, "dp", ("role", "tensor"), None),
        P(None, "dp", None, None),
    )
    return jax.shard_map(
        local, mesh=mesh, in_specs=placed, out_specs=P(("role", "tensor"), "dp"), check_vma=False
    )
```

```python
import jax
import jax.numpy as jnp
from jax import lax
from jax.sharding import PartitionSpec as P

LAT = 512
EXPERTS = 16
TEN = 3


SCORE_SCALE = 0.07216878364870323
NORM_EPS = 1e-06
MASKED = -1e30
RT = ("role", "tensor")


def rms_rows(input_rows, norm_gain):
    wide = input_rows.astype(jnp.float32)
    scale = lax.rsqrt(jnp.mean(wide * wide, axis=-1, keepdims=True) + NORM_EPS)
    return (wide * scale * norm_gain.astype(jnp.float32)).astype(jnp.bfloat16)


def slot_table(routes, expert, capacity):
    hit = jnp.any(routes == expert, axis=-1).astype(jnp.int32)
    earlier = jnp.cumsum(hit, axis=-1) - hit
    slot_ids = jnp.arange(capacity, dtype=jnp.int32)
    return (hit[..., None, :] > 0) & (earlier[..., None, :] == slot_ids[:, None])


def local(
    queries,
    latent_cache,
    new_latent,
    cache_lengths,
    value_proj,
    out_proj,
    residual,
    norm_gain,
    routes,
    gate_values,
    tenant_ids,
    expert_gate_weight,
    expert_up_weight,
    expert_down_weight,
    left_delta_factor,
    factor_right,
):
    n_slices = lax.axis_size(RT)
    slice_idx = lax.axis_index(RT)
    group_rows = residual.shape[0]
    capacity = 5 * group_rows // 8
    model_width = expert_down_weight.shape[2]
    col_width = model_width // n_slices

    expert = lax.axis_index("dp")
    labels = jnp.arange(EXPERTS, dtype=jnp.int32)
    table = slot_table(routes, labels[:, None, None], capacity)
    mine = lax.dynamic_index_in_dim(table, expert, 0, keepdims=False)
    mine_owner = jnp.sum(mine.astype(jnp.int32) * tenant_ids[None, :], axis=1)
    hidden_slice = expert_down_weight.shape[1]
    down_local = expert_down_weight[0].reshape(hidden_slice, n_slices, col_width)
    down_local = jnp.transpose(down_local, (1, 0, 2))
    left_local = left_delta_factor[:, 0]
    tenants, _, rank = left_local.shape
    left_local = jnp.transpose(left_local, (1, 0, 2)).reshape(hidden_slice, tenants * rank)
    left_all = lax.all_gather(left_local, RT, axis=0, tiled=True)
    down_pack = down_local
    pack_width = down_pack.shape[2]
    info = mine_owner.astype(jnp.bfloat16)
    info_rows = jnp.zeros((8, pack_width), jnp.bfloat16).at[0, : info.shape[0]].set(info)
    info_rows = jnp.broadcast_to(info_rows[None], (n_slices, 8, pack_width))
    down_pack = jnp.concatenate([down_pack, info_rows], axis=1)
    down_pack = lax.all_to_all(down_pack, RT, split_axis=0, concat_axis=0, tiled=True)
    right_w = lax.dynamic_slice_in_dim(factor_right[:, 0], slice_idx * col_width, col_width, 2)

    seq_count, context, width = latent_cache.shape
    local_heads = queries.shape[1]
    paired = queries.reshape(seq_count, 2, local_heads, width)
    scores = (
        jnp.einsum("sqhd,spd->sqhp", paired, latent_cache, preferred_element_type=jnp.float32)
        * SCORE_SCALE
    )
    present = jnp.arange(context, dtype=jnp.int32)[None, :] < cache_lengths[:, None]
    scores = jnp.where(present[:, None, None, :], scores, MASKED)
    fresh_keys = new_latent.reshape(seq_count, 2, width)
    fresh = (
        jnp.einsum("sqhd,skd->sqhk", paired, fresh_keys, preferred_element_type=jnp.float32)
        * SCORE_SCALE
    )
    causal = jnp.arange(2)[:, None] >= jnp.arange(2)[None, :]
    fresh = jnp.where(causal[None, :, None, :], fresh, MASKED)
    top = jnp.maximum(jnp.max(scores, axis=3), jnp.max(fresh, axis=3))[..., None]
    weights = jnp.exp(scores - top)
    fresh_weights = jnp.exp(fresh - top)
    total = jnp.sum(weights, axis=3) + jnp.sum(fresh_weights, axis=3)
    summed = jnp.einsum(
        "sqhp,spd->sqhd",
        weights.astype(jnp.bfloat16),
        latent_cache[:, :, :LAT],
        preferred_element_type=jnp.float32,
    )
    summed = summed + jnp.einsum(
        "sqhk,skd->sqhd",
        fresh_weights.astype(jnp.bfloat16),
        fresh_keys[:, :, :LAT],
        preferred_element_type=jnp.float32,
    )
    attended = (
        (summed / total[..., None]).astype(jnp.bfloat16).reshape(seq_count * 2, local_heads, LAT)
    )
    by_head = lax.all_to_all(attended, "tensor", split_axis=1, concat_axis=0, tiled=True)
    head_values = jnp.einsum(
        "thl,hlv->thv", by_head, value_proj, preferred_element_type=jnp.float32
    ).astype(jnp.bfloat16)
    head_values = head_values.reshape(
        head_values.shape[0], head_values.shape[1] * head_values.shape[2]
    )
    all_values = lax.all_gather(head_values, "dp", axis=0, tiled=True)
    owners = down_pack[:, hidden_slice, :capacity].astype(jnp.int32).reshape(n_slices * capacity)
    down_pack = down_pack[:, :hidden_slice].reshape(n_slices * hidden_slice, pack_width)
    down_w = down_pack[:, :col_width]
    left_w = left_all.reshape(n_slices * hidden_slice, tenants, rank)
    down_w, left_w, owners, all_values = lax.optimization_barrier((down_w, left_w, owners, all_values))
    partial = jnp.dot(all_values, out_proj, preferred_element_type=jnp.float32)
    half = partial.shape[0] // 2
    role_idx = lax.axis_index("role")
    keep = lax.dynamic_slice_in_dim(partial, role_idx * half, half, 0)
    give = lax.dynamic_slice_in_dim(partial, (1 - role_idx) * half, half, 0)
    partial = keep + lax.ppermute(give, "role", [(0, 1), (1, 0)])
    n_tensor = lax.axis_size("tensor")
    partial = partial.reshape(n_tensor, partial.shape[0] // n_tensor, partial.shape[1])
    partial = lax.all_to_all(partial.astype(jnp.bfloat16), "tensor", split_axis=0, concat_axis=0, tiled=True)
    attention = jnp.sum(partial.astype(jnp.float32), axis=0)
    mixed_in = lax.optimization_barrier(
        (residual.astype(jnp.float32) + attention).astype(jnp.bfloat16)
    )

    n_dp = lax.axis_size("dp")
    spread = jnp.broadcast_to(mixed_in[None], (n_dp,) + mixed_in.shape)
    full_rows = lax.all_to_all(spread, "dp", split_axis=0, concat_axis=0, tiled=True)
    full_rows = full_rows.reshape(-1, group_rows, mixed_in.shape[1])
    full_rows = jnp.transpose(full_rows, (1, 0, 2)).reshape(group_rows, model_width)
    normed = rms_rows(full_rows, norm_gain)
    picked = jnp.dot(
        mine.astype(jnp.bfloat16), normed, preferred_element_type=jnp.float32
    ).astype(jnp.bfloat16)
    collected_rows = lax.all_gather(picked, RT, axis=0, tiled=True)
    gate_scores = jnp.dot(collected_rows, expert_gate_weight[0], preferred_element_type=jnp.float32)
    upper_bound = jnp.dot(collected_rows, expert_up_weight[0], preferred_element_type=jnp.float32)
    hidden = (jax.nn.silu(gate_scores) * upper_bound).astype(jnp.bfloat16)

    gathered = lax.all_gather(hidden, RT, axis=0, tiled=False)
    down_w = down_w.reshape(n_slices, hidden_slice, col_width)
    left_w = left_w.reshape(n_slices, hidden_slice, tenants, rank)
    base_output = jnp.einsum("jsh,jhc->sc", gathered, down_w, preferred_element_type=jnp.float32)
    owner_mask = (owners[:, None] == jnp.arange(TEN, dtype=jnp.int32)[None, :]).astype(jnp.float32)
    mixing = jnp.einsum(
        "jsf,jftr->str", gathered, left_w, preferred_element_type=jnp.float32
    ) * owner_mask[:, :, None]
    delta = jnp.einsum(
        "str,trd->sd", mixing, right_w.astype(jnp.float32), precision=lax.Precision.HIGHEST
    )
    expert_out = (base_output - delta).astype(jnp.bfloat16)
    expert_out = expert_out.reshape(n_slices, capacity, col_width)
    by_group = lax.all_to_all(expert_out, RT, split_axis=0, concat_axis=0, tiled=True)
    by_expert = lax.all_to_all(by_group, "dp", split_axis=0, concat_axis=0, tiled=True)

    chosen = (routes[:, :, None] == labels[None, None, :]).astype(jnp.float32)
    gate_of = jnp.sum(gate_values[:, :, None] * chosen, axis=1)
    weighting = table.astype(jnp.float32) * gate_of.T[:, None, :]
    expert_part = jnp.einsum(
        "ecg,ecd->gd", weighting, by_expert.astype(jnp.float32), precision=lax.Precision.HIGHEST
    )
    return (mixed_in.astype(jnp.float32) + expert_part).astype(jnp.bfloat16)


def solution(mesh):
    placed = (
        P(("dp", "tensor"), "role", None),
        P(("dp", "tensor"), None, None),
        P(("dp", "tensor"), None),
        P(("dp", "tensor")),
        P(("role", "tensor"), None, None),
        P(("role", "tensor"), "dp"),
        P(("role", "tensor"), "dp"),
        P(),
        P(("role", "tensor"), None),
        P(("role", "tensor"), None),
        P(("role", "tensor")),
        P("dp", None, ("role", "tensor")),
        P("dp", None, ("role", "tensor")),
        P("dp", ("role", "tensor"), None),
        P(None, "dp", ("role", "tensor"), None),
        P(None, "dp", None, None),
    )
    return jax.shard_map(
        local, mesh=mesh, in_specs=placed, out_specs=P(("role", "tensor"), "dp"), check_vma=False
    )
```

```python
import jax
import jax.numpy as jnp
from jax import lax
from jax.sharding import PartitionSpec as P

LAT = 512
EXPERTS = 16
TEN = 3


SCORE_SCALE = 0.07216878364870323
NORM_EPS = 1e-06
MASKED = -1e30
RT = ("role", "tensor")


def rms_rows(input_rows, norm_gain):
    wide = input_rows.astype(jnp.float32)
    scale = lax.rsqrt(jnp.mean(wide * wide, axis=-1, keepdims=True) + NORM_EPS)
    return (wide * scale * norm_gain.astype(jnp.float32)).astype(jnp.bfloat16)


def slot_table(routes, expert, capacity):
    hit = jnp.any(routes == expert, axis=-1).astype(jnp.int32)
    earlier = jnp.cumsum(hit, axis=-1) - hit
    slot_ids = jnp.arange(capacity, dtype=jnp.int32)
    return (hit[..., None, :] > 0) & (earlier[..., None, :] == slot_ids[:, None])


def local(
    queries,
    latent_cache,
    new_latent,
    cache_lengths,
    value_proj,
    out_proj,
    residual,
    norm_gain,
    routes,
    gate_values,
    tenant_ids,
    expert_gate_weight,
    expert_up_weight,
    expert_down_weight,
    left_delta_factor,
    factor_right,
):
    n_slices = lax.axis_size(RT)
    slice_idx = lax.axis_index(RT)
    group_rows = residual.shape[0]
    capacity = 5 * group_rows // 8
    model_width = expert_down_weight.shape[2]
    col_width = model_width // n_slices

    expert = lax.axis_index("dp")
    labels = jnp.arange(EXPERTS, dtype=jnp.int32)
    table = slot_table(routes, labels[:, None, None], capacity)
    mine = lax.dynamic_index_in_dim(table, expert, 0, keepdims=False)
    mine_owner = jnp.sum(mine.astype(jnp.int32) * tenant_ids[None, :], axis=1)
    hidden_slice = expert_down_weight.shape[1]
    down_local = expert_down_weight[0].reshape(hidden_slice, n_slices, col_width)
    down_local = jnp.transpose(down_local, (1, 0, 2))
    left_local = left_delta_factor[:, 0]
    tenants, _, rank = left_local.shape
    left_local = jnp.transpose(left_local, (1, 0, 2)).reshape(1, hidden_slice, tenants * rank)
    left_local = jnp.broadcast_to(left_local, (n_slices, hidden_slice, tenants * rank))
    down_pack = jnp.concatenate([down_local, left_local], axis=2)
    pack_width = down_pack.shape[2]
    info = mine_owner.astype(jnp.bfloat16)
    info_rows = jnp.zeros((8, pack_width), jnp.bfloat16).at[0, : info.shape[0]].set(info)
    info_rows = jnp.broadcast_to(info_rows[None], (n_slices, 8, pack_width))
    down_pack = jnp.concatenate([down_pack, info_rows], axis=1)
    down_pack = lax.all_to_all(down_pack, RT, split_axis=0, concat_axis=0, tiled=True)
    right_w = lax.dynamic_slice_in_dim(factor_right[:, 0], slice_idx * col_width, col_width, 2)

    seq_count, context, width = latent_cache.shape
    local_heads = queries.shape[1]
    paired = queries.reshape(seq_count, 2, local_heads, width)
    scores = (
        jnp.einsum("sqhd,spd->sqhp", paired, latent_cache, preferred_element_type=jnp.float32)
        * SCORE_SCALE
    )
    present = jnp.arange(context, dtype=jnp.int32)[None, :] < cache_lengths[:, None]
    scores = jnp.where(present[:, None, None, :], scores, MASKED)
    fresh_keys = new_latent.reshape(seq_count, 2, width)
    fresh = (
        jnp.einsum("sqhd,skd->sqhk", paired, fresh_keys, preferred_element_type=jnp.float32)
        * SCORE_SCALE
    )
    causal = jnp.arange(2)[:, None] >= jnp.arange(2)[None, :]
    fresh = jnp.where(causal[None, :, None, :], fresh, MASKED)
    top = jnp.maximum(jnp.max(scores, axis=3), jnp.max(fresh, axis=3))[..., None]
    weights = jnp.exp(scores - top)
    fresh_weights = jnp.exp(fresh - top)
    total = jnp.sum(weights, axis=3) + jnp.sum(fresh_weights, axis=3)
    summed = jnp.einsum(
        "sqhp,spd->sqhd",
        weights.astype(jnp.bfloat16),
        latent_cache[:, :, :LAT],
        preferred_element_type=jnp.float32,
    )
    summed = summed + jnp.einsum(
        "sqhk,skd->sqhd",
        fresh_weights.astype(jnp.bfloat16),
        fresh_keys[:, :, :LAT],
        preferred_element_type=jnp.float32,
    )
    attended = (
        (summed / total[..., None]).astype(jnp.bfloat16).reshape(seq_count * 2, local_heads, LAT)
    )
    by_head = lax.all_to_all(attended, "tensor", split_axis=1, concat_axis=0, tiled=True)
    head_values = jnp.einsum(
        "thl,hlv->thv", by_head, value_proj, preferred_element_type=jnp.float32
    ).astype(jnp.bfloat16)
    head_values = head_values.reshape(
        head_values.shape[0], head_values.shape[1] * head_values.shape[2]
    )
    all_values = lax.all_gather(head_values, "dp", axis=0, tiled=True)
    owners = down_pack[:, hidden_slice, :capacity].astype(jnp.int32).reshape(n_slices * capacity)
    down_pack = down_pack[:, :hidden_slice].reshape(n_slices * hidden_slice, pack_width)
    down_w = down_pack[:, :col_width]
    left_w = down_pack[:, col_width:].reshape(n_slices * hidden_slice, tenants, rank)
    down_w, left_w, owners, all_values = lax.optimization_barrier((down_w, left_w, owners, all_values))
    partial = jnp.dot(all_values, out_proj, preferred_element_type=jnp.float32)
    half = partial.shape[0] // 2
    role_idx = lax.axis_index("role")
    keep = lax.dynamic_slice_in_dim(partial, role_idx * half, half, 0)
    give = lax.dynamic_slice_in_dim(partial, (1 - role_idx) * half, half, 0)
    partial = keep + lax.ppermute(give.astype(jnp.bfloat16), "role", [(0, 1), (1, 0)]).astype(jnp.float32)
    n_tensor = lax.axis_size("tensor")
    partial = partial.reshape(n_tensor, partial.shape[0] // n_tensor, partial.shape[1])
    partial = lax.all_to_all(partial.astype(jnp.bfloat16), "tensor", split_axis=0, concat_axis=0, tiled=True)
    attention = jnp.sum(partial.astype(jnp.float32), axis=0)
    mixed_in = lax.optimization_barrier(
        (residual.astype(jnp.float32) + attention).astype(jnp.bfloat16)
    )

    n_dp = lax.axis_size("dp")
    spread = jnp.broadcast_to(mixed_in[None], (n_dp,) + mixed_in.shape)
    full_rows = lax.all_to_all(spread, "dp", split_axis=0, concat_axis=0, tiled=True)
    full_rows = full_rows.reshape(-1, group_rows, mixed_in.shape[1])
    full_rows = jnp.transpose(full_rows, (1, 0, 2)).reshape(group_rows, model_width)
    normed = rms_rows(full_rows, norm_gain)
    picked = jnp.dot(
        mine.astype(jnp.bfloat16), normed, preferred_element_type=jnp.float32
    ).astype(jnp.bfloat16)
    collected_rows = lax.all_gather(picked, RT, axis=0, tiled=True)
    gate_scores = jnp.dot(collected_rows, expert_gate_weight[0], preferred_element_type=jnp.float32)
    upper_bound = jnp.dot(collected_rows, expert_up_weight[0], preferred_element_type=jnp.float32)
    hidden = (jax.nn.silu(gate_scores) * upper_bound).astype(jnp.bfloat16)

    gathered = lax.all_gather(hidden, RT, axis=0, tiled=False)
    down_w = down_w.reshape(n_slices, hidden_slice, col_width)
    left_w = left_w.reshape(n_slices, hidden_slice, tenants, rank)
    base_output = jnp.einsum("jsh,jhc->sc", gathered, down_w, preferred_element_type=jnp.float32)
    owner_mask = (owners[:, None] == jnp.arange(TEN, dtype=jnp.int32)[None, :]).astype(jnp.float32)
    mixing = jnp.einsum(
        "jsf,jftr->str", gathered, left_w, preferred_element_type=jnp.float32
    ) * owner_mask[:, :, None]
    delta = jnp.einsum(
        "str,trd->sd", mixing, right_w.astype(jnp.float32), precision=lax.Precision.HIGHEST
    )
    expert_out = (base_output - delta).astype(jnp.bfloat16)
    expert_out = expert_out.reshape(n_slices, capacity, col_width)
    by_group = lax.all_to_all(expert_out, RT, split_axis=0, concat_axis=0, tiled=True)
    by_expert = lax.all_to_all(by_group, "dp", split_axis=0, concat_axis=0, tiled=True)

    chosen = (routes[:, :, None] == labels[None, None, :]).astype(jnp.float32)
    gate_of = jnp.sum(gate_values[:, :, None] * chosen, axis=1)
    weighting = table.astype(jnp.float32) * gate_of.T[:, None, :]
    expert_part = jnp.einsum(
        "ecg,ecd->gd", weighting, by_expert.astype(jnp.float32), precision=lax.Precision.HIGHEST
    )
    return (mixed_in.astype(jnp.float32) + expert_part).astype(jnp.bfloat16)


def solution(mesh):
    placed = (
        P(("dp", "tensor"), "role", None),
        P(("dp", "tensor"), None, None),
        P(("dp", "tensor"), None),
        P(("dp", "tensor")),
        P(("role", "tensor"), None, None),
        P(("role", "tensor"), "dp"),
        P(("role", "tensor"), "dp"),
        P(),
        P(("role", "tensor"), None),
        P(("role", "tensor"), None),
        P(("role", "tensor")),
        P("dp", None, ("role", "tensor")),
        P("dp", None, ("role", "tensor")),
        P("dp", ("role", "tensor"), None),
        P(None, "dp", ("role", "tensor"), None),
        P(None, "dp", None, None),
    )
    return jax.shard_map(
        local, mesh=mesh, in_specs=placed, out_specs=P(("role", "tensor"), "dp"), check_vma=False
    )
```
